512 devices in a mesh: nodes: 128 (over z, y, core), rep: 4 (over x).
Axes of the slice: x: 4, y: 8, z: 8, core: 2. Of those that a mesh axis runs over, the one named last changes fastest.
Arguments:
- memory: float32 [65536, 512], P('nodes'), may hold values from -16 to 16
- last_tick: int32 [65536], P('nodes'), may hold values from 0 to 499
- src_local: int32 [65536], P(('nodes', 'rep')), may hold values from 0 to 511
- dst_owner: int32 [65536, 1], P(('nodes', 'rep')), may hold values from 0 to 127; in each aligned block of 128 rows (0 to 127, 128 to 255, ...) at most 2 rows name the same one
- dst_local: int32 [65536], P(('nodes', 'rep')), may hold values from 0 to 511
- event_tick: int32 [65536], P(('nodes', 'rep')), may hold values from 500 to 999
- nbr_owner: int32 [65536, 16, 1], P(('nodes', 'rep')), may hold values from 0 to 127; in each aligned block of 2048 rows (0 to 2047, 2048 to 4095, ..., all dimensions but the last counted through in order) at most 32 rows name the same one
- nbr_local: int32 [65536, 16], P(('nodes', 'rep')), may hold values from 0 to 511
- nbr_tick: int32 [65536, 16], P(('nodes', 'rep')), may hold values from 0 to 499
- freq: float32 [128], replicated, may hold values from 0.002 to 0.5
- phase: float32 [128], replicated, may hold values from -3.140625 to 3.140625
- w_message: bfloat16 [1152, 512], replicated, may hold values from -0.1875 to 0.1875
- gru_input: float32 [3, 512, 512], P(None, None, 'rep'), may hold values from -0.5 to 0.5
- gru_hidden: float32 [3, 512, 512], P(None, None, 'rep'), may hold values from -0.25 to 0.25
- gru_bias: float32 [4, 512], P(None, 'rep'), may hold values from -3 to 3
- w_query: bfloat16 [512, 512], replicated, may hold values from -1 to 1
- w_keyval_mem: bfloat16 [512, 1024], replicated, may hold values from -0.25 to 0.25
- w_keyval_time: bfloat16 [128, 1024], replicated, may hold values from -0.5 to 0.5
Outputs:
- new_memory: float32 [65536, 512], P('nodes', 'rep')
- embed: bfloat16 [65536, 512], P(('nodes', 'rep'))
The draws below stay inside these ranges and needn't reach their ends.
Inputs may be any that keep to these rules, and one draw needn't show every extreme that they name: `dst_owner`: on one device no owner is named by more than 2 events. `nbr_owner`: on one device no owner is named by more than 32 neighbour entries.
All inputs are finite; a program needn't handle non-finite values.
Results may differ from the reference program's by a relative error of at most 0.012.
The reference program's roundings to bfloat16 on the way (of `mem_half`, `upd_half`, `query` and `kv_mem`) count: a program that leaves them out, or rounds other values in their place, can miss the bound.
Values may be sent and summed in bfloat16 or wider, within the bound.
No kernel may reach another device: no remote copies, remote signals or barrier semaphores. Data moves between devices by JAX's collectives and lax.ppermute only.
A program may use at most 128 MiB of HBM per device.

```python
import math
import jax
import jax.numpy as jnp
import numpy as np
from jax import lax

M = 512
MSG = 512
TE = 128
HEADS = 8
HEAD_DIM = 64
NBR = 16
EV_DEV = 128
ROWS_DEV = 512
E = 512
CAPD = 2
CAPN = 32
EVENTS = 65536
ROWS = 65536
N_NODES = 128
N_REP = 4


def draw_memory(key, part):
    first = jax.random.fold_in(jax.random.fold_in(key, 7), 0)
    base = jnp.clip(jax.random.normal(first, (ROWS, M), jnp.float32), -4.0, 4.0)
    return base


def place_ends(drawn, rng, low, high):
    extent = drawn.shape
    place = [jax.random.randint(jax.random.fold_in(rng, axis), (), 0, extent[axis]) for axis in range(len(extent))]
    drawn = drawn.at[tuple(place)].set(low)
    longest = extent.index(max(extent))
    place[longest] = (place[longest] + 1) % extent[longest]
    return drawn.at[tuple(place)].set(high)


def steps_of(rng, extent, shards, least, high):
    gain, own = 1.0, jax.random.fold_in(rng, 6)
    for dim, parts in shards:
        heights = jnp.exp(jax.random.uniform(jax.random.fold_in(own, dim), (parts,), jnp.float32, least / len(shards), high / len(shards)))
        gain = gain * jnp.repeat(heights, extent[dim] // parts).reshape([-1 if axis == dim else 1 for axis in range(len(extent))])
    return gain


def assign_block(key, own, number, rows, number_of, top, reach, skew):
    ranking = jax.random.permutation(key, number_of)
    heavy_load, common = portions_of(number_of, rows * top, reach, skew, True), portions_of(number_of, rows * top, reach, skew, False)
    places = jnp.arange(number_of)

    def named(lengths, offset_by):
        used = int((lengths > 0).sum())
        fixed = max(1, used // 4)
        passed = fixed + (places - fixed + offset_by * (used - fixed)) % max(1, number_of - fixed)
        return jnp.zeros((number_of,), jnp.int32).at[ranking[jnp.where(places < fixed, places, passed)]].set(jnp.asarray(lengths, jnp.int32))

    lengths = jnp.where(number % 4 == 0, named(heavy_load, number // 4), named(common, number - number // 4 - 1))
    mixed = jax.random.permutation(jax.random.fold_in(own, 3), number_of)
    source_of, sink = mixed[0:number_of // 2 * 2:2], mixed[1:number_of // 2 * 2:2]
    slack = jnp.minimum(lengths[source_of] - 1, reach - lengths[sink]) // 2
    slack = jnp.where((source_of == ranking[0]) | (sink == ranking[0]) | (lengths[sink] == 0), 0, jnp.maximum(slack, 0))
    passed = jax.random.randint(jax.random.fold_in(own, 4), (number_of // 2,), 0, 1 << 20) % (slack + 1)
    lengths = lengths.at[source_of].add(-passed).at[sink].add(passed)
    labels = jnp.searchsorted(jnp.cumsum(lengths), jnp.arange(rows * top), side="right").astype(jnp.int32)
    table = labels.reshape(top, rows).T
    table = table[jax.random.permutation(jax.random.fold_in(own, 1), rows)]
    offset_by = jax.random.randint(jax.random.fold_in(own, 2), (rows, 1), 0, top)
    return jnp.take_along_axis(table, (jnp.arange(top)[None, :] + offset_by) % top, axis=1)


def portions_of(amount, total, limit, lean, full):
    loads = [(1 << 20) // math.isqrt(standing ** lean) + 1 for standing in range(1, amount + 1)]
    largest = limit if full else min(limit, max(-(-total // amount), total * loads[0] // sum(loads)))
    least = 1 if total - largest >= amount - 1 else 0
    holding, spare = [largest] + [least] * (amount - 1), total - largest - least * (amount - 1)
    while spare > 0:
        candidates = [i for i in range(1, amount) if holding[i] < largest] or [i for i in range(1, amount) if holding[i] < limit]
        pool, remaining = sum([loads[i] for i in candidates]), spare
        for i in candidates:
            addition = min(limit - holding[i], max(1, remaining * loads[i] // pool), spare)
            holding[i] = holding[i] + addition
            spare = spare - addition
    return np.array(holding)


def normal_values(own_key, extent, width, limit, pieces=(), kind=jnp.bfloat16):
    drawn = jax.random.normal(own_key, extent, jnp.float32) * width
    if len(pieces) > 0:
        drawn = steps_of(own_key, extent, pieces, -0.22, 0.18) * drawn
    return jnp.clip(drawn, min=-limit, max=limit).astype(kind)


def setup_inputs(seed: int = 0) -> dict:
    arg_keys = jax.random.split(jax.random.key(seed), 19)
    memory = draw_memory(jax.random.fold_in(arg_keys[18], 71), 0)
    last_tick = place_ends(jax.random.randint(arg_keys[1], (ROWS,), 0, 500), jax.random.fold_in(arg_keys[1], 1), 0, 499).astype(jnp.int32)
    src_local = place_ends(jax.random.randint(arg_keys[2], (EVENTS,), 0, ROWS_DEV), jax.random.fold_in(arg_keys[2], 1), 0, ROWS_DEV - 1).astype(jnp.int32)
    dst_owner_keys = jax.random.split(jax.random.fold_in(arg_keys[3], 1), EVENTS // EV_DEV)
    dst_owner_turns = jax.random.permutation(jax.random.fold_in(arg_keys[3], 3), EVENTS // EV_DEV)
    dst_owner = jax.vmap(lambda own, number: assign_block(jax.random.fold_in(arg_keys[3], 2), own, number, EV_DEV, N_NODES, 1, CAPD, 2))(dst_owner_keys, dst_owner_turns).reshape((EVENTS, 1))
    dst_local = place_ends(jax.random.randint(arg_keys[4], (EVENTS,), 0, ROWS_DEV), jax.random.fold_in(arg_keys[4], 1), 0, ROWS_DEV - 1).astype(jnp.int32)
    event_tick = place_ends(jax.random.randint(arg_keys[5], (EVENTS,), 500, 1000), jax.random.fold_in(arg_keys[5], 1), 500, 999).astype(jnp.int32)
    nbr_owner_keys = jax.random.split(jax.random.fold_in(arg_keys[6], 1), EVENTS * NBR // (EV_DEV * NBR))
    nbr_owner_turns = jax.random.permutation(jax.random.fold_in(arg_keys[6], 3), EVENTS * NBR // (EV_DEV * NBR))
    nbr_owner = jax.vmap(lambda own, number: assign_block(jax.random.fold_in(arg_keys[6], 2), own, number, EV_DEV * NBR, N_NODES, 1, CAPN, 2))(nbr_owner_keys, nbr_owner_turns).reshape((EVENTS, NBR, 1))
    nbr_local = place_ends(jax.random.randint(arg_keys[7], (EVENTS, NBR), 0, ROWS_DEV), jax.random.fold_in(arg_keys[7], 1), 0, ROWS_DEV - 1).astype(jnp.int32)
    nbr_tick = place_ends(jax.random.randint(arg_keys[8], (EVENTS, NBR), 0, 500), jax.random.fold_in(arg_keys[8], 1), 0, 499).astype(jnp.int32)
    freq = jnp.clip(jnp.exp(jax.random.uniform(arg_keys[9], (TE,), jnp.float32, math.log(0.002), math.log(0.5))), 0.002, 0.5)
    phase = jnp.clip(jax.random.uniform(arg_keys[10], (TE,), jnp.float32, -3.140625, 3.140625), -3.140625, 3.140625)
    w_message = normal_values(arg_keys[11], (2 * M + TE, MSG), (2 * M + TE) ** -0.5, 0.1875)
    gru_input = normal_values(arg_keys[12], (3, MSG, M), (MSG // 4) ** -0.5, 0.5, ((2, 4),), jnp.float32)
    gru_hidden = normal_values(arg_keys[13], (3, M, M), M ** -0.5, 0.25, ((2, 4),), jnp.float32)
    gru_bias = normal_values(arg_keys[14], (4, M), 0.5, 3.0, ((1, 4),), jnp.float32)
    w_query = normal_values(arg_keys[15], (M, E), (M // 16) ** -0.5, 1.0)
    w_keyval_mem = normal_values(arg_keys[16], (M, 2 * E), M ** -0.5, 0.25)
    w_keyval_time = normal_values(arg_keys[17], (TE, 2 * E), TE ** -0.5, 0.5)
    return dict(memory=memory, last_tick=last_tick, src_local=src_local, dst_owner=dst_owner, dst_local=dst_local, event_tick=event_tick, nbr_owner=nbr_owner, nbr_local=nbr_local, nbr_tick=nbr_tick, freq=freq, phase=phase, w_message=w_message, gru_input=gru_input, gru_hidden=gru_hidden, gru_bias=gru_bias, w_query=w_query, w_keyval_mem=w_keyval_mem, w_keyval_time=w_keyval_time)


def encode(gaps, freq, phase):
    return jnp.cos(gaps[..., None] * freq + phase)

def reference(memory, last_tick, src_local, dst_owner, dst_local, event_tick, nbr_owner, nbr_local, nbr_tick, freq, phase, w_message, gru_input, gru_hidden, gru_bias, w_query, w_keyval_mem, w_keyval_time):
    events = src_local.shape[0]
    total_rows = memory.shape[0]
    group = jnp.arange(events, dtype=jnp.int32) // (EV_DEV * N_REP)
    source = (group * ROWS_DEV + src_local).astype(jnp.int32)
    target = (dst_owner[:, 0] * ROWS_DEV + dst_local).astype(jnp.int32)
    mem_half = memory.astype(jnp.bfloat16)
    ticks = event_tick.astype(jnp.float32)
    src_time = encode(ticks - last_tick[source].astype(jnp.float32), freq, phase).astype(jnp.bfloat16)
    dst_time = encode(ticks - last_tick[target].astype(jnp.float32), freq, phase).astype(jnp.bfloat16)
    src_in = jnp.concatenate([mem_half[source], mem_half[target], src_time], axis=1)
    dst_in = jnp.concatenate([mem_half[target], mem_half[source], dst_time], axis=1)
    msg_src = jax.nn.silu(jnp.dot(src_in, w_message, preferred_element_type=jnp.float32)).astype(jnp.bfloat16)
    msg_dst = jax.nn.silu(jnp.dot(dst_in, w_message, preferred_element_type=jnp.float32)).astype(jnp.bfloat16)
    msg_src = lax.optimization_barrier(msg_src).astype(jnp.float32)
    msg_dst = lax.optimization_barrier(msg_dst).astype(jnp.float32)
    sums = jax.ops.segment_sum(msg_src, source, total_rows) + jax.ops.segment_sum(msg_dst, target, total_rows)
    ones = jnp.ones((events,), jnp.float32)
    counts = jax.ops.segment_sum(ones, source, total_rows) + jax.ops.segment_sum(ones, target, total_rows)
    mean = sums / jnp.maximum(counts, 1.0)[:, None]
    highest = lax.Precision.HIGHEST
    a_parts = [jnp.dot(mean, gru_input[g], precision=highest) for g in range(3)]
    b_parts = [jnp.dot(memory, gru_hidden[g], precision=highest) for g in range(3)]
    update = jax.nn.sigmoid(a_parts[0] + b_parts[0] + gru_bias[0])
    reset = jax.nn.sigmoid(a_parts[1] + b_parts[1] + gru_bias[1])
    cand = jnp.tanh(a_parts[2] + gru_bias[2] + reset * (b_parts[2] + gru_bias[3]))
    fresh = (1.0 - update) * cand + update * memory
    new_memory = jnp.where((counts > 0.0)[:, None], fresh, memory)
    upd_half = new_memory.astype(jnp.bfloat16)
    query = jnp.dot(upd_half[source], w_query, preferred_element_type=jnp.float32).astype(jnp.bfloat16)
    query = lax.optimization_barrier(query).astype(jnp.float32)
    blocks = events // EV_DEV
    attn_width = HEADS * HEAD_DIM

    def attend(inputs):
        q_block, own_block, loc_block, ntick_block, tick_block = inputs
        nbr = (own_block[:, :, 0] * ROWS_DEV + loc_block).astype(jnp.int32)
        rows_block = upd_half[nbr.reshape(-1)]
        kv_mem = jnp.dot(rows_block, w_keyval_mem, preferred_element_type=jnp.float32).astype(jnp.bfloat16)
        kv_mem = lax.optimization_barrier(kv_mem).astype(jnp.float32)
        gaps = tick_block.astype(jnp.float32)[:, None] - ntick_block.astype(jnp.float32)
        time_enc = encode(gaps, freq, phase).reshape(-1, freq.shape[0]).astype(jnp.bfloat16)
        kv_time = jnp.dot(time_enc, w_keyval_time, preferred_element_type=jnp.float32)
        keyval = (kv_mem + kv_time).reshape(EV_DEV, NBR, 2, HEADS, HEAD_DIM)
        qh = q_block.reshape(EV_DEV, HEADS, HEAD_DIM)
        scores = jnp.einsum('ehd,ejhd->ehj', qh, keyval[:, :, 0]) / math.sqrt(HEAD_DIM)
        weights = jax.nn.softmax(scores, axis=-1)
        out = jnp.einsum('ehj,ejhd->ehd', weights, keyval[:, :, 1])
        return out.reshape(EV_DEV, attn_width).astype(jnp.bfloat16)
    embed = lax.map(attend, (query.reshape(blocks, EV_DEV, attn_width), nbr_owner.reshape(blocks, EV_DEV, NBR, 1), nbr_local.reshape(blocks, EV_DEV, NBR), nbr_tick.reshape(blocks, EV_DEV, NBR), event_tick.reshape(blocks, EV_DEV)))
    return (new_memory, embed.reshape(events, attn_width))
```

```python
import math

import jax
import jax.numpy as jnp
from jax import lax
from jax.sharding import PartitionSpec as P

HEADS = 8
HEAD_DIM = 64


def encode(gaps, freq, phase):
    return jnp.cos(gaps[..., None] * freq + phase)


def place(owner, groups, capacity):
    onehot = (owner[:, None] == jnp.arange(groups, dtype=jnp.int32)[None, :]).astype(jnp.int32)
    before = jnp.cumsum(onehot, axis=0) - onehot
    return owner * capacity + jnp.sum(before * onehot, axis=1)


def select_rows(ids, table):
    hits = (ids[:, None] == jnp.arange(table.shape[0], dtype=jnp.int32)[None, :]).astype(table.dtype)
    return jnp.dot(hits, table, preferred_element_type=jnp.float32).astype(table.dtype)


def on_device(
    memory,
    last_tick,
    src_local,
    dst_owner,
    dst_local,
    event_tick,
    nbr_owner,
    nbr_local,
    nbr_tick,
    freq,
    phase,
    w_message,
    gru_input,
    gru_hidden,
    gru_bias,
    w_query,
    w_keyval_mem,
    w_keyval_time,
):
    groups = lax.axis_size("nodes")
    reps = lax.axis_size("rep")
    events = src_local.shape[0]
    rows_here = memory.shape[0]
    width_m = memory.shape[1]
    neighbours = nbr_local.shape[1]
    dst_cap = max(2, 2 * events // groups)
    nbr_cap = 2 * events * neighbours // groups
    dst_slot = place(dst_owner[:, 0], groups, dst_cap)
    nbr_slot = place(nbr_owner.reshape(-1), groups, nbr_cap)
    mem_half = memory.astype(jnp.bfloat16)
    near_rows = mem_half[src_local]
    near_ticks = last_tick[src_local]
    ticks = event_tick.astype(jnp.float32)

    req = jnp.stack([dst_local, event_tick, near_ticks], axis=1)
    req_ints = (
        jnp.full((groups * dst_cap, 3), -1, jnp.int32)
        .at[dst_slot]
        .set(req)
        .reshape(groups, dst_cap * 3)
    )
    nbr_ids = (
        jnp.full((groups * nbr_cap,), -1, jnp.int32)
        .at[nbr_slot]
        .set(nbr_local.reshape(-1))
        .reshape(groups, nbr_cap)
    )
    req_rows = (
        jnp.zeros((groups * dst_cap, width_m), jnp.bfloat16)
        .at[dst_slot]
        .set(near_rows)
        .reshape(groups, dst_cap, width_m)
    )
    ints_out = jnp.concatenate([req_ints, nbr_ids], axis=1)
    ints_in = lax.all_to_all(ints_out, "nodes", split_axis=0, concat_axis=0, tiled=True)
    rows_in = lax.all_to_all(req_rows, "nodes", split_axis=0, concat_axis=0, tiled=True)
    got = ints_in[:, : dst_cap * 3].reshape(groups * dst_cap, 3)
    got_nbr = ints_in[:, dst_cap * 3 :]
    got_dst = got[:, 0]
    got_tick = got[:, 1].astype(jnp.float32)
    got_src_tick = got[:, 2].astype(jnp.float32)
    safe_dst = jnp.maximum(got_dst, 0)
    far_src = rows_in.reshape(-1, width_m)
    own_dst = mem_half[safe_dst]
    own_dst_tick = last_tick[safe_dst].astype(jnp.float32)

    src_time = encode(got_tick - got_src_tick, freq, phase).astype(jnp.bfloat16)
    dst_time = encode(got_tick - own_dst_tick, freq, phase).astype(jnp.bfloat16)
    slots = far_src.shape[0]
    stacked = jnp.concatenate(
        [
            jnp.concatenate([far_src, own_dst, src_time], axis=1),
            jnp.concatenate([own_dst, far_src, dst_time], axis=1),
        ],
        axis=0,
    )
    messages = jax.nn.silu(jnp.dot(stacked, w_message, preferred_element_type=jnp.float32)).astype(
        jnp.bfloat16
    )
    msg_src_slots = messages[:slots]
    msg_dst = messages[slots:]
    back = lax.all_to_all(
        msg_src_slots.reshape(groups, dst_cap, -1), "nodes", split_axis=0, concat_axis=0, tiled=True
    )
    msg_src = back.reshape(-1, back.shape[2])[dst_slot]

    local_msgs = jnp.concatenate([msg_src, msg_dst], axis=0)
    local_ids = jnp.concatenate([src_local, got_dst], axis=0)
    all_msgs = [local_msgs]
    all_ids = [local_ids]
    for shift in range(1, reps):
        pairs = [(i, (i + shift) % reps) for i in range(reps)]
        all_msgs.append(lax.ppermute(local_msgs, "rep", pairs))
        all_ids.append(lax.ppermute(local_ids, "rep", pairs))
    all_msgs = jnp.concatenate(all_msgs, axis=0)
    all_ids = jnp.concatenate(all_ids, axis=0)
    row_ids = jnp.arange(rows_here, dtype=jnp.int32)[:, None]
    hits = row_ids == all_ids[None, :]
    sums = jnp.dot(hits.astype(jnp.bfloat16), all_msgs, preferred_element_type=jnp.float32)
    counts = jnp.sum(hits.astype(jnp.float32), axis=1)

    unit_width = gru_bias.shape[1]
    start = lax.axis_index("rep") * unit_width
    state_part = lax.dynamic_slice_in_dim(memory, start, unit_width, 1)
    mean = sums / jnp.maximum(counts, 1.0)[:, None]
    highest = lax.Precision.HIGHEST
    a_parts = jnp.einsum("rk,gku->gru", mean, gru_input, precision=highest)
    b_parts = jnp.einsum("rk,gku->gru", memory, gru_hidden, precision=highest)
    update = jax.nn.sigmoid(a_parts[0] + b_parts[0] + gru_bias[0])
    reset = jax.nn.sigmoid(a_parts[1] + b_parts[1] + gru_bias[1])
    cand = jnp.tanh(a_parts[2] + gru_bias[2] + reset * (b_parts[2] + gru_bias[3]))
    fresh = (1.0 - update) * cand + update * state_part
    new_part = jnp.where((counts > 0.0)[:, None], fresh, state_part)
    updated = lax.all_gather(new_part.astype(jnp.bfloat16), "rep", axis=1, tiled=True)
    served = select_rows(got_nbr.reshape(-1), updated).reshape(groups, nbr_cap, -1)
    returned = lax.all_to_all(served, "nodes", split_axis=0, concat_axis=0, tiled=True)
    fetched = returned.reshape(-1, updated.shape[1])[nbr_slot]
    kv_mem = jnp.dot(fetched, w_keyval_mem, preferred_element_type=jnp.float32).astype(jnp.bfloat16)
    kv_mem = lax.optimization_barrier(kv_mem).astype(jnp.float32)
    gaps = ticks[:, None] - nbr_tick.astype(jnp.float32)
    time_enc = encode(gaps, freq, phase).reshape(-1, freq.shape[0]).astype(jnp.bfloat16)
    kv_time = jnp.dot(time_enc, w_keyval_time, preferred_element_type=jnp.float32)
    keyval = (kv_mem + kv_time).reshape(events, neighbours, 2, HEADS, HEAD_DIM)
    query = jnp.dot(updated[src_local], w_query, preferred_element_type=jnp.float32).astype(
        jnp.bfloat16
    )
    query = lax.optimization_barrier(query).astype(jnp.float32).reshape(events, HEADS, HEAD_DIM)
    scores = jnp.einsum("ehd,ejhd->ehj", query, keyval[:, :, 0]) / math.sqrt(HEAD_DIM)
    weights = jax.nn.softmax(scores, axis=-1)
    mixed = jnp.einsum("ehj,ejhd->ehd", weights, keyval[:, :, 1])
    embed = mixed.reshape(events, HEADS * HEAD_DIM).astype(jnp.bfloat16)
    return (new_part, embed)


def solution(mesh):
    placed = (
        P("nodes", None),
        P("nodes"),
        P(("nodes", "rep")),
        P(("nodes", "rep"), None),
        P(("nodes", "rep")),
        P(("nodes", "rep")),
        P(("nodes", "rep"), None, None),
        P(("nodes", "rep"), None),
        P(("nodes", "rep"), None),
        P(),
        P(),
        P(),
        P(None, None, "rep"),
        P(None, None, "rep"),
        P(None, "rep"),
        P(),
        P(),
        P(),
    )
    return jax.shard_map(
        on_device,
        mesh=mesh,
        in_specs=placed,
        out_specs=(P("nodes", "rep"), P(("nodes", "rep"), None)),
        check_vma=False,
    )
```

```python
import math

import jax
import jax.numpy as jnp
from jax import lax
from jax.sharding import PartitionSpec as P

HEADS = 8
HEAD_DIM = 64


def encode(gaps, freq, phase):
    return jnp.cos(gaps[..., None] * freq + phase)


def place(owner, groups, capacity):
    onehot = (owner[:, None] == jnp.arange(groups, dtype=jnp.int32)[None, :]).astype(jnp.int32)
    before = jnp.cumsum(onehot, axis=0) - onehot
    return owner * capacity + jnp.sum(before * onehot, axis=1)


def select_rows(ids, table):
    hits = (ids[:, None] == jnp.arange(table.shape[0], dtype=jnp.int32)[None, :]).astype(table.dtype)
    return jnp.dot(hits, table, preferred_element_type=jnp.float32).astype(table.dtype)


def on_device(
    memory,
    last_tick,
    src_local,
    dst_owner,
    dst_local,
    event_tick,
    nbr_owner,
    nbr_local,
    nbr_tick,
    freq,
    phase,
    w_message,
    gru_input,
    gru_hidden,
    gru_bias,
    w_query,
    w_keyval_mem,
    w_keyval_time,
):
    groups = lax.axis_size("nodes")
    reps = lax.axis_size("rep")
    events = src_local.shape[0]
    rows_here = memory.shape[0]
    width_m = memory.shape[1]
    neighbours = nbr_local.shape[1]
    dst_cap = max(2, 2 * events // groups)
    nbr_cap = 2 * events * neighbours // groups
    dst_slot = place(dst_owner[:, 0], groups, dst_cap)
    nbr_slot = place(nbr_owner.reshape(-1), groups, nbr_cap)
    mem_half = memory.astype(jnp.bfloat16)
    near_rows = mem_half[src_local]
    near_ticks = last_tick[src_local]
    ticks = event_tick.astype(jnp.float32)

    def split(v):
        return jnp.stack([v // 32, v % 32], axis=1).astype(jnp.bfloat16)

    def join(pairs):
        pairs = pairs.astype(jnp.int32)
        return pairs[..., 0] * 32 + pairs[..., 1]

    slots = groups * dst_cap
    extra = 128
    ev_ints = jnp.concatenate(
        [split(dst_local + 1), split(event_tick), split(near_ticks)], axis=1
    )
    ev_payload = jnp.concatenate(
        [near_rows, ev_ints, jnp.zeros((events, extra - 6), jnp.bfloat16)], axis=1
    )
    slot_hits = (jnp.arange(slots, dtype=jnp.int32)[:, None] == dst_slot[None, :]).astype(jnp.bfloat16)
    req = jnp.dot(slot_hits, ev_payload, preferred_element_type=jnp.float32).astype(jnp.bfloat16)
    nbr_hits = (
        jnp.arange(groups * nbr_cap, dtype=jnp.int32)[:, None] == nbr_slot[None, :]
    ).astype(jnp.bfloat16)
    nbr_req = jnp.dot(
        nbr_hits, split(nbr_local.reshape(-1) + 1), preferred_element_type=jnp.float32
    ).astype(jnp.bfloat16)
    nbr_req = nbr_req.reshape(groups, dst_cap, nbr_cap * 2 // dst_cap)
    req = req.reshape(groups, dst_cap, width_m + extra)
    req = jnp.concatenate(
        [
            req[:, :, : width_m + 6],
            nbr_req,
            jnp.zeros((groups, dst_cap, extra - 6 - nbr_req.shape[2]), jnp.bfloat16),
        ],
        axis=2,
    )
    got_all = lax.all_to_all(req, "nodes", split_axis=0, concat_axis=0, tiled=True)
    got_rows = got_all[:, :, : width_m + 6].reshape(slots, width_m + 6)
    far_src = got_rows[:, :width_m]
    got_ints = join(got_rows[:, width_m:].reshape(slots, 3, 2))
    got_dst = got_ints[:, 0] - 1
    got_tick = got_ints[:, 1].astype(jnp.float32)
    got_src_tick = got_ints[:, 2].astype(jnp.float32)
    nbr_width = nbr_req.shape[2]
    got_nbr = join(
        got_all[:, :, width_m + 6 : width_m + 6 + nbr_width].reshape(groups, nbr_cap, 2)
    ) - 1
    safe_dst = jnp.maximum(got_dst, 0)
    own_dst = mem_half[safe_dst]
    own_dst_tick = last_tick[safe_dst].astype(jnp.float32)

    src_time = encode(got_tick - got_src_tick, freq, phase).astype(jnp.bfloat16)
    dst_time = encode(got_tick - own_dst_tick, freq, phase).astype(jnp.bfloat16)
    stacked = jnp.concatenate(
        [
            jnp.concatenate([far_src, own_dst, src_time], axis=1),
            jnp.concatenate([own_dst, far_src, dst_time], axis=1),
        ],
        axis=0,
    )
    messages = jax.nn.silu(jnp.dot(stacked, w_message, preferred_element_type=jnp.float32)).astype(
        jnp.bfloat16
    )
    msg_src_slots = messages[:slots]
    msg_dst = messages[slots:]
    back = lax.all_to_all(
        msg_src_slots.reshape(groups, dst_cap, -1), "nodes", split_axis=0, concat_axis=0, tiled=True
    )
    msg_src = back.reshape(-1, back.shape[2])[dst_slot]

    def spread(value):
        parts = [value]
        for shift in range(1, reps):
            pairs = [(i, (i + shift) % reps) for i in range(reps)]
            parts.append(lax.ppermute(value, "rep", pairs))
        return jnp.concatenate(parts, axis=0)

    all_msgs = jnp.concatenate([spread(msg_dst), spread(msg_src)], axis=0)
    all_ids = jnp.concatenate([spread(got_dst), spread(src_local)], axis=0)
    row_ids = jnp.arange(rows_here, dtype=jnp.int32)[:, None]
    hits = row_ids == all_ids[None, :]
    sums = jnp.dot(hits.astype(jnp.bfloat16), all_msgs, preferred_element_type=jnp.float32)
    counts = jnp.sum(hits.astype(jnp.float32), axis=1)

    unit_width = gru_bias.shape[1]
    start = lax.axis_index("rep") * unit_width
    state_part = lax.dynamic_slice_in_dim(memory, start, unit_width, 1)
    mean = sums / jnp.maximum(counts, 1.0)[:, None]
    highest = lax.Precision.HIGHEST
    a_parts = jnp.einsum("rk,gku->gru", mean, gru_input, precision=highest)
    b_parts = jnp.einsum("rk,gku->gru", memory, gru_hidden, precision=highest)
    update = jax.nn.sigmoid(a_parts[0] + b_parts[0] + gru_bias[0])
    reset = jax.nn.sigmoid(a_parts[1] + b_parts[1] + gru_bias[1])
    cand = jnp.tanh(a_parts[2] + gru_bias[2] + reset * (b_parts[2] + gru_bias[3]))
    fresh = (1.0 - update) * cand + update * state_part
    new_part = jnp.where((counts > 0.0)[:, None], fresh, state_part)
    updated = lax.all_gather(new_part.astype(jnp.bfloat16), "rep", axis=1, tiled=True)
    served = select_rows(got_nbr.reshape(-1), updated).reshape(groups, nbr_cap, -1)
    returned = lax.all_to_all(served, "nodes", split_axis=0, concat_axis=0, tiled=True)
    fetched = returned.reshape(-1, updated.shape[1])[nbr_slot]
    kv_mem = jnp.dot(fetched, w_keyval_mem, preferred_element_type=jnp.float32).astype(jnp.bfloat16)
    kv_mem = lax.optimization_barrier(kv_mem).astype(jnp.float32)
    gaps = ticks[:, None] - nbr_tick.astype(jnp.float32)
    time_enc = encode(gaps, freq, phase).reshape(-1, freq.shape[0]).astype(jnp.bfloat16)
    kv_time = jnp.dot(time_enc, w_keyval_time, preferred_element_type=jnp.float32)
    keyval = (kv_mem + kv_time).reshape(events, neighbours, 2, HEADS * HEAD_DIM)
    keys = keyval[:, :, 0]
    values = keyval[:, :, 1]
    query = jnp.dot(updated[src_local], w_query, preferred_element_type=jnp.float32).astype(
        jnp.bfloat16
    )
    query = lax.optimization_barrier(query).astype(jnp.float32)
    prod = (keys * query[:, None, :]).reshape(events, neighbours, HEADS, HEAD_DIM)
    scores = jnp.sum(prod, axis=-1) / math.sqrt(HEAD_DIM)
    weights = jax.nn.softmax(scores, axis=1)
    spread_w = jnp.repeat(weights, HEAD_DIM, axis=2)
    mixed = jnp.sum(spread_w * values, axis=1)
    embed = mixed.astype(jnp.bfloat16)
    return (new_part, embed)


def solution(mesh):
    placed = (
        P("nodes", None),
        P("nodes"),
        P(("nodes", "rep")),
        P(("nodes", "rep"), None),
        P(("nodes", "rep")),
        P(("nodes", "rep")),
        P(("nodes", "rep"), None, None),
        P(("nodes", "rep"), None),
        P(("nodes", "rep"), None),
        P(),
        P(),
        P(),
        P(None, None, "rep"),
        P(None, None, "rep"),
        P(None, "rep"),
        P(),
        P(),
        P(),
    )
    return jax.shard_map(
        on_device,
        mesh=mesh,
        in_specs=placed,
        out_specs=(P("nodes", "rep"), P(("nodes", "rep"), None)),
        check_vma=False,
    )
```

```python
import math

import jax
import jax.numpy as jnp
from jax import lax
from jax.experimental import pallas as pl
from jax.experimental.pallas import tpu as pltpu
from jax.sharding import PartitionSpec as P

HEADS = 8
HEAD_DIM = 64


def encode(gaps, freq, phase):
    return jnp.cos(gaps[..., None] * freq + phase)


def place(owner, groups, capacity):
    onehot = (owner[:, None] == jnp.arange(groups, dtype=jnp.int32)[None, :]).astype(jnp.int32)
    before = jnp.cumsum(onehot, axis=0) - onehot
    return owner * capacity + jnp.sum(before * onehot, axis=1)


def select_rows(ids, table):
    hits = (ids[:, None] == jnp.arange(table.shape[0], dtype=jnp.int32)[None, :]).astype(table.dtype)
    return jnp.dot(hits, table, preferred_element_type=jnp.float32).astype(table.dtype)


def attend_kernel(fetched_ref, tenc_ref, q_ref, wm_ref, wt_ref, out_ref):
    f32, bf16 = jnp.float32, jnp.bfloat16
    block = q_ref.shape[0]
    rows = fetched_ref.shape[0]
    nbrs = rows // block
    width = q_ref.shape[1]
    kv_mem = jnp.dot(fetched_ref[...], wm_ref[...], preferred_element_type=f32).astype(bf16)
    kv_time = jnp.dot(tenc_ref[...], wt_ref[...], preferred_element_type=f32)
    keyval = kv_mem.astype(f32) + kv_time
    keys = keyval[:, :width]
    values = keyval[:, width:]
    query = q_ref[...].astype(f32)
    prod = (keys.reshape(block, nbrs, width) * query[:, None, :]).reshape(rows, width)
    lane = lax.broadcasted_iota(jnp.int32, (width, 128), 0)
    col = lax.broadcasted_iota(jnp.int32, (width, 128), 1)
    head_of = (lane // HEAD_DIM == col).astype(f32)
    highest = lax.Precision.HIGHEST
    scores = jnp.dot(prod, head_of, preferred_element_type=f32, precision=highest)
    scores = (scores / math.sqrt(HEAD_DIM)).reshape(block, nbrs, 128)
    top = jnp.max(scores, axis=1, keepdims=True)
    ex = jnp.exp(scores - top)
    weights = (ex / jnp.sum(ex, axis=1, keepdims=True)).reshape(rows, 128)
    row = lax.broadcasted_iota(jnp.int32, (128, width), 0)
    lane2 = lax.broadcasted_iota(jnp.int32, (128, width), 1)
    head_to = (lane2 // HEAD_DIM == row).astype(f32)
    spread = jnp.dot(weights, head_to, preferred_element_type=f32, precision=highest)
    mixed = jnp.sum((spread * values).reshape(block, nbrs, width), axis=1)
    out_ref[...] = mixed.astype(out_ref.dtype)


def attend(fetched, time_enc, query, w_keyval_mem, w_keyval_time, block=16):
    events, width = query.shape
    nbrs = fetched.shape[0] // events
    rows = block * nbrs
    return pl.pallas_call(
        attend_kernel,
        grid=(events // block,),
        in_specs=[
            pl.BlockSpec((rows, fetched.shape[1]), lambda i: (i, 0)),
            pl.BlockSpec((rows, time_enc.shape[1]), lambda i: (i, 0)),
            pl.BlockSpec((block, width), lambda i: (i, 0)),
            pl.BlockSpec(w_keyval_mem.shape, lambda i: (0, 0)),
            pl.BlockSpec(w_keyval_time.shape, lambda i: (0, 0)),
        ],
        out_specs=pl.BlockSpec((block, width), lambda i: (i, 0)),
        out_shape=jax.ShapeDtypeStruct((events, width), jnp.bfloat16),
    )(fetched, time_enc, query, w_keyval_mem, w_keyval_time)


def on_device(
    memory,
    last_tick,
    src_local,
    dst_owner,
    dst_local,
    event_tick,
    nbr_owner,
    nbr_local,
    nbr_tick,
    freq,
    phase,
    w_message,
    gru_input,
    gru_hidden,
    gru_bias,
    w_query,
    w_keyval_mem,
    w_keyval_time,
):
    groups = lax.axis_size("nodes")
    reps = lax.axis_size("rep")
    events = src_local.shape[0]
    rows_here = memory.shape[0]
    width_m = memory.shape[1]
    neighbours = nbr_local.shape[1]
    dst_cap = max(2, 2 * events // groups)
    nbr_cap = 2 * events * neighbours // groups
    dst_slot = place(dst_owner[:, 0], groups, dst_cap)
    nbr_slot = place(nbr_owner.reshape(-1), groups, nbr_cap)
    mem_half = memory.astype(jnp.bfloat16)
    near_rows = mem_half[src_local]
    near_ticks = last_tick[src_local]
    ticks = event_tick.astype(jnp.float32)

    req = jnp.stack([dst_local, event_tick, near_ticks], axis=1)
    req_ints = (
        jnp.full((groups * dst_cap, 3), -1, jnp.int32)
        .at[dst_slot]
        .set(req)
        .reshape(groups, dst_cap * 3)
    )
    nbr_ids = (
        jnp.full((groups * nbr_cap,), -1, jnp.int32)
        .at[nbr_slot]
        .set(nbr_local.reshape(-1))
        .reshape(groups, nbr_cap)
    )
    req_rows = (
        jnp.zeros((groups * dst_cap, width_m), jnp.bfloat16)
        .at[dst_slot]
        .set(near_rows)
        .reshape(groups, dst_cap, width_m)
    )
    ints_out = jnp.concatenate([req_ints, nbr_ids], axis=1)
    ints_in = lax.all_to_all(ints_out, "nodes", split_axis=0, concat_axis=0, tiled=True)
    rows_in = lax.all_to_all(req_rows, "nodes", split_axis=0, concat_axis=0, tiled=True)
    got = ints_in[:, : dst_cap * 3].reshape(groups * dst_cap, 3)
    got_nbr = ints_in[:, dst_cap * 3 :]
    got_dst = got[:, 0]
    got_tick = got[:, 1].astype(jnp.float32)
    got_src_tick = got[:, 2].astype(jnp.float32)
    safe_dst = jnp.maximum(got_dst, 0)
    far_src = rows_in.reshape(-1, width_m)
    own_dst = mem_half[safe_dst]
    own_dst_tick = last_tick[safe_dst].astype(jnp.float32)

    src_time = encode(got_tick - got_src_tick, freq, phase).astype(jnp.bfloat16)
    dst_time = encode(got_tick - own_dst_tick, freq, phase).astype(jnp.bfloat16)
    slots = far_src.shape[0]
    stacked = jnp.concatenate(
        [
            jnp.concatenate([far_src, own_dst, src_time], axis=1),
            jnp.concatenate([own_dst, far_src, dst_time], axis=1),
        ],
        axis=0,
    )
    messages = jax.nn.silu(jnp.dot(stacked, w_message, preferred_element_type=jnp.float32)).astype(
        jnp.bfloat16
    )
    msg_src_slots = messages[:slots]
    msg_dst = messages[slots:]
    back = lax.all_to_all(
        msg_src_slots.reshape(groups, dst_cap, -1), "nodes", split_axis=0, concat_axis=0, tiled=True
    )
    msg_src = back.reshape(-1, back.shape[2])[dst_slot]

    local_msgs = jnp.concatenate([msg_src, msg_dst], axis=0)
    local_ids = jnp.concatenate([src_local, got_dst], axis=0)
    all_msgs = [local_msgs]
    all_ids = [local_ids]
    for shift in range(1, reps):
        pairs = [(i, (i + shift) % reps) for i in range(reps)]
        all_msgs.append(lax.ppermute(local_msgs, "rep", pairs))
        all_ids.append(lax.ppermute(local_ids, "rep", pairs))
    all_msgs = jnp.concatenate(all_msgs, axis=0)
    all_ids = jnp.concatenate(all_ids, axis=0)
    row_ids = jnp.arange(rows_here, dtype=jnp.int32)[:, None]
    hits = row_ids == all_ids[None, :]
    sums = jnp.dot(hits.astype(jnp.bfloat16), all_msgs, preferred_element_type=jnp.float32)
    counts = jnp.sum(hits.astype(jnp.float32), axis=1)

    unit_width = gru_bias.shape[1]
    start = lax.axis_index("rep") * unit_width
    state_part = lax.dynamic_slice_in_dim(memory, start, unit_width, 1)
    mean = sums / jnp.maximum(counts, 1.0)[:, None]
    highest = lax.Precision.HIGHEST
    a_parts = jnp.einsum("rk,gku->gru", mean, gru_input, precision=highest)
    b_parts = jnp.einsum("rk,gku->gru", memory, gru_hidden, precision=highest)
    update = jax.nn.sigmoid(a_parts[0] + b_parts[0] + gru_bias[0])
    reset = jax.nn.sigmoid(a_parts[1] + b_parts[1] + gru_bias[1])
    cand = jnp.tanh(a_parts[2] + gru_bias[2] + reset * (b_parts[2] + gru_bias[3]))
    fresh = (1.0 - update) * cand + update * state_part
    new_part = jnp.where((counts > 0.0)[:, None], fresh, state_part)
    updated = lax.all_gather(new_part.astype(jnp.bfloat16), "rep", axis=1, tiled=True)
    served = select_rows(got_nbr.reshape(-1), updated).reshape(groups, nbr_cap, -1)
    returned = lax.all_to_all(served, "nodes", split_axis=0, concat_axis=0, tiled=True)
    fetched = returned.reshape(-1, updated.shape[1])[nbr_slot]
    gaps = ticks[:, None] - nbr_tick.astype(jnp.float32)
    time_enc = encode(gaps, freq, phase).reshape(-1, freq.shape[0]).astype(jnp.bfloat16)
    query = jnp.dot(updated[src_local], w_query, preferred_element_type=jnp.float32).astype(
        jnp.bfloat16
    )
    embed = attend(fetched, time_enc, query, w_keyval_mem, w_keyval_time)
    return (new_part, embed)


def solution(mesh):
    placed = (
        P("nodes", None),
        P("nodes"),
        P(("nodes", "rep")),
        P(("nodes", "rep"), None),
        P(("nodes", "rep")),
        P(("nodes", "rep")),
        P(("nodes", "rep"), None, None),
        P(("nodes", "rep"), None),
        P(("nodes", "rep"), None),
        P(),
        P(),
        P(),
        P(None, None, "rep"),
        P(None, None, "rep"),
        P(None, "rep"),
        P(),
        P(),
        P(),
    )
    return jax.shard_map(
        on_device,
        mesh=mesh,
        in_specs=placed,
        out_specs=(P("nodes", "rep"), P(("nodes", "rep"), None)),
        check_vma=False,
    )
```

```python
import math

import jax
import jax.numpy as jnp
from jax import lax
from jax.experimental import pallas as pl
from jax.experimental.pallas import tpu as pltpu
from jax.sharding import PartitionSpec as P

HEADS = 8
HEAD_DIM = 64


def encode(gaps, freq, phase):
    return jnp.cos(gaps[..., None] * freq + phase)


def place(owner, groups, capacity):
    onehot = (owner[:, None] == jnp.arange(groups, dtype=jnp.int32)[None, :]).astype(jnp.int32)
    before = jnp.cumsum(onehot, axis=0) - onehot
    rank = jnp.sum(before * onehot, axis=1)
    return owner * capacity + rank, onehot, rank


def split_pairs(v):
    return (v // 32).astype(jnp.bfloat16), (v % 32).astype(jnp.bfloat16)


def scatter_ids(onehot, rank, values, capacity):
    hi, lo = split_pairs(values + 1)
    at_rank = rank[:, None] == jnp.arange(capacity, dtype=jnp.int32)[None, :]
    cols = jnp.concatenate(
        [jnp.where(at_rank, hi[:, None], 0.0), jnp.where(at_rank, lo[:, None], 0.0)], axis=1
    ).astype(jnp.bfloat16)
    table = jnp.dot(onehot.T.astype(jnp.bfloat16), cols, preferred_element_type=jnp.float32)
    table = table.astype(jnp.int32)
    return table[:, :capacity] * 32 + table[:, capacity:] - 1


def select_rows(ids, table):
    hits = (ids[:, None] == jnp.arange(table.shape[0], dtype=jnp.int32)[None, :]).astype(table.dtype)
    return jnp.dot(hits, table, preferred_element_type=jnp.float32).astype(table.dtype)


def attend_kernel(fetched_ref, tenc_ref, q_ref, wm_ref, wt_ref, out_ref):
    f32, bf16 = jnp.float32, jnp.bfloat16
    block = q_ref.shape[0]
    rows = fetched_ref.shape[0]
    nbrs = rows // block
    width = q_ref.shape[1]
    kv_mem = jnp.dot(fetched_ref[...], wm_ref[...], preferred_element_type=f32).astype(bf16)
    kv_time = jnp.dot(tenc_ref[...], wt_ref[...], preferred_element_type=f32)
    keyval = kv_mem.astype(f32) + kv_time
    keys = keyval[:, :width]
    values = keyval[:, width:]
    query = q_ref[...].astype(f32)
    prod = (keys.reshape(block, nbrs, width) * query[:, None, :]).reshape(rows, width)
    lane = lax.broadcasted_iota(jnp.int32, (width, 128), 0)
    col = lax.broadcasted_iota(jnp.int32, (width, 128), 1)
    head_of = (lane // HEAD_DIM == col).astype(f32)
    highest = lax.Precision.HIGHEST
    scores = jnp.dot(prod, head_of, preferred_element_type=f32, precision=highest)
    scores = (scores / math.sqrt(HEAD_DIM)).reshape(block, nbrs, 128)
    top = jnp.max(scores, axis=1, keepdims=True)
    ex = jnp.exp(scores - top)
    weights = (ex / jnp.sum(ex, axis=1, keepdims=True)).reshape(rows, 128)
    row = lax.broadcasted_iota(jnp.int32, (128, width), 0)
    lane2 = lax.broadcasted_iota(jnp.int32, (128, width), 1)
    head_to = (lane2 // HEAD_DIM == row).astype(f32)
    spread = jnp.dot(weights, head_to, preferred_element_type=f32, precision=highest)
    mixed = jnp.sum((spread * values).reshape(block, nbrs, width), axis=1)
    out_ref[...] = mixed.astype(out_ref.dtype)


def attend(fetched, time_enc, query, w_keyval_mem, w_keyval_time, block=16):
    events, width = query.shape
    nbrs = fetched.shape[0] // events
    rows = block * nbrs
    return pl.pallas_call(
        attend_kernel,
        grid=(events // block,),
        in_specs=[
            pl.BlockSpec((rows, fetched.shape[1]), lambda i: (i, 0)),
            pl.BlockSpec((rows, time_enc.shape[1]), lambda i: (i, 0)),
            pl.BlockSpec((block, width), lambda i: (i, 0)),
            pl.BlockSpec(w_keyval_mem.shape, lambda i: (0, 0)),
            pl.BlockSpec(w_keyval_time.shape, lambda i: (0, 0)),
        ],
        out_specs=pl.BlockSpec((block, width), lambda i: (i, 0)),
        out_shape=jax.ShapeDtypeStruct((events, width), jnp.bfloat16),
    )(fetched, time_enc, query, w_keyval_mem, w_keyval_time)


def on_device(
    memory,
    last_tick,
    src_local,
    dst_owner,
    dst_local,
    event_tick,
    nbr_owner,
    nbr_local,
    nbr_tick,
    freq,
    phase,
    w_message,
    gru_input,
    gru_hidden,
    gru_bias,
    w_query,
    w_keyval_mem,
    w_keyval_time,
):
    groups = lax.axis_size("nodes")
    reps = lax.axis_size("rep")
    events = src_local.shape[0]
    rows_here = memory.shape[0]
    width_m = memory.shape[1]
    neighbours = nbr_local.shape[1]
    dst_cap = max(2, 2 * events // groups)
    nbr_cap = 2 * events * neighbours // groups
    dst_slot, _, _ = place(dst_owner[:, 0], groups, dst_cap)
    nbr_slot, nbr_hot, nbr_rank = place(nbr_owner.reshape(-1), groups, nbr_cap)
    mem_half = memory.astype(jnp.bfloat16)
    near_rows = mem_half[src_local]
    near_ticks = last_tick[src_local]
    ticks = event_tick.astype(jnp.float32)

    req = jnp.stack([dst_local, event_tick, near_ticks], axis=1)
    req_ints = (
        jnp.full((groups * dst_cap, 3), -1, jnp.int32)
        .at[dst_slot]
        .set(req)
        .reshape(groups, dst_cap * 3)
    )
    nbr_ids = scatter_ids(nbr_hot, nbr_rank, nbr_local.reshape(-1), nbr_cap)
    req_rows = (
        jnp.zeros((groups * dst_cap, width_m), jnp.bfloat16)
        .at[dst_slot]
        .set(near_rows)
        .reshape(groups, dst_cap, width_m)
    )
    ints_out = jnp.concatenate([req_ints, nbr_ids], axis=1)
    ints_in = lax.all_to_all(ints_out, "nodes", split_axis=0, concat_axis=0, tiled=True)
    rows_in = lax.all_to_all(req_rows, "nodes", split_axis=0, concat_axis=0, tiled=True)
    got = ints_in[:, : dst_cap * 3].reshape(groups * dst_cap, 3)
    got_nbr = ints_in[:, dst_cap * 3 :]
    got_dst = got[:, 0]
    got_tick = got[:, 1].astype(jnp.float32)
    got_src_tick = got[:, 2].astype(jnp.float32)
    safe_dst = jnp.maximum(got_dst, 0)
    far_src = rows_in.reshape(-1, width_m)
    own_dst = mem_half[safe_dst]
    own_dst_tick = last_tick[safe_dst].astype(jnp.float32)

    src_time = encode(got_tick - got_src_tick, freq, phase).astype(jnp.bfloat16)
    dst_time = encode(got_tick - own_dst_tick, freq, phase).astype(jnp.bfloat16)
    slots = far_src.shape[0]
    stacked = jnp.concatenate(
        [
            jnp.concatenate([far_src, own_dst, src_time], axis=1),
            jnp.concatenate([own_dst, far_src, dst_time], axis=1),
        ],
        axis=0,
    )
    messages = jax.nn.silu(jnp.dot(stacked, w_message, preferred_element_type=jnp.float32)).astype(
        jnp.bfloat16
    )
    msg_src_slots = messages[:slots]
    msg_dst = messages[slots:]
    back = lax.all_to_all(
        msg_src_slots.reshape(groups, dst_cap, -1), "nodes", split_axis=0, concat_axis=0, tiled=True
    )
    msg_src = back.reshape(-1, back.shape[2])[dst_slot]

    local_msgs = jnp.concatenate([msg_src, msg_dst], axis=0)
    local_ids = jnp.concatenate([src_local, got_dst], axis=0)
    id_hi, id_lo = split_pairs(local_ids + 1)
    id_rows = -(-2 * local_ids.shape[0] // width_m)
    id_rows = -(-id_rows // 16) * 16
    id_block = jnp.concatenate(
        [id_hi, id_lo, jnp.zeros((id_rows * width_m - 2 * local_ids.shape[0],), jnp.bfloat16)]
    ).reshape(id_rows, width_m)
    payload = jnp.concatenate([local_msgs, id_block], axis=0)
    parts = [payload]
    for shift in range(1, reps):
        pairs = [(i, (i + shift) % reps) for i in range(reps)]
        parts.append(lax.ppermute(payload, "rep", pairs))
    count = local_msgs.shape[0]
    all_msgs = jnp.concatenate([p[:count] for p in parts], axis=0)
    coded = jnp.stack([p[count:].reshape(-1)[: 2 * count] for p in parts]).astype(jnp.int32)
    all_ids = (coded[:, :count] * 32 + coded[:, count:] - 1).reshape(-1)
    row_ids = jnp.arange(rows_here, dtype=jnp.int32)[:, None]
    hits = row_ids == all_ids[None, :]
    sums = jnp.dot(hits.astype(jnp.bfloat16), all_msgs, preferred_element_type=jnp.float32)
    counts = jnp.sum(hits.astype(jnp.float32), axis=1)

    unit_width = gru_bias.shape[1]
    start = lax.axis_index("rep") * unit_width
    state_part = lax.dynamic_slice_in_dim(memory, start, unit_width, 1)
    mean = sums / jnp.maximum(counts, 1.0)[:, None]
    highest = lax.Precision.HIGHEST
    a_parts = jnp.einsum("rk,gku->gru", mean, gru_input, precision=highest)
    b_parts = jnp.einsum("rk,gku->gru", memory, gru_hidden, precision=highest)
    update = jax.nn.sigmoid(a_parts[0] + b_parts[0] + gru_bias[0])
    reset = jax.nn.sigmoid(a_parts[1] + b_parts[1] + gru_bias[1])
    cand = jnp.tanh(a_parts[2] + gru_bias[2] + reset * (b_parts[2] + gru_bias[3]))
    fresh = (1.0 - update) * cand + update * state_part
    new_part = jnp.where((counts > 0.0)[:, None], fresh, state_part)
    updated = lax.all_gather(new_part.astype(jnp.bfloat16), "rep", axis=1, tiled=True)
    served = select_rows(got_nbr.reshape(-1), updated).reshape(groups, nbr_cap, -1)
    returned = lax.all_to_all(served, "nodes", split_axis=0, concat_axis=0, tiled=True)
    fetched = returned.reshape(-1, updated.shape[1])[nbr_slot]
    gaps = ticks[:, None] - nbr_tick.astype(jnp.float32)
    time_enc = encode(gaps, freq, phase).reshape(-1, freq.shape[0]).astype(jnp.bfloat16)
    query = jnp.dot(updated[src_local], w_query, preferred_element_type=jnp.float32).astype(
        jnp.bfloat16
    )
    embed = attend(fetched, time_enc, query, w_keyval_mem, w_keyval_time)
    return (new_part, embed)


def solution(mesh):
    placed = (
        P("nodes", None),
        P("nodes"),
        P(("nodes", "rep")),
        P(("nodes", "rep"), None),
        P(("nodes", "rep")),
        P(("nodes", "rep")),
        P(("nodes", "rep"), None, None),
        P(("nodes", "rep"), None),
        P(("nodes", "rep"), None),
        P(),
        P(),
        P(),
        P(None, None, "rep"),
        P(None, None, "rep"),
        P(None, "rep"),
        P(),
        P(),
        P(),
    )
    return jax.shard_map(
        on_device,
        mesh=mesh,
        in_specs=placed,
        out_specs=(P("nodes", "rep"), P(("nodes", "rep"), None)),
        check_vma=False,
    )
```

```python
import math

import jax
import jax.numpy as jnp
from jax import lax
from jax.experimental import pallas as pl
from jax.experimental.pallas import tpu as pltpu
from jax.sharding import PartitionSpec as P

HEADS = 8
HEAD_DIM = 64


def encode(gaps, freq, phase):
    return jnp.cos(gaps[..., None] * freq + phase)


def place(owner, groups, capacity):
    onehot = (owner[:, None] == jnp.arange(groups, dtype=jnp.int32)[None, :]).astype(jnp.int32)
    before = jnp.cumsum(onehot, axis=0) - onehot
    rank = jnp.sum(before * onehot, axis=1)
    return owner * capacity + rank, onehot, rank


def split_pairs(v):
    return (v // 32).astype(jnp.bfloat16), (v % 32).astype(jnp.bfloat16)


def scatter_ids(onehot, rank, values, capacity):
    hi, lo = split_pairs(values + 1)
    at_rank = rank[:, None] == jnp.arange(capacity, dtype=jnp.int32)[None, :]
    cols = jnp.concatenate(
        [jnp.where(at_rank, hi[:, None], 0.0), jnp.where(at_rank, lo[:, None], 0.0)], axis=1
    ).astype(jnp.bfloat16)
    table = jnp.dot(onehot.T.astype(jnp.bfloat16), cols, preferred_element_type=jnp.float32)
    table = table.astype(jnp.int32)
    return table[:, :capacity] * 32 + table[:, capacity:] - 1


def select_rows(ids, table):
    hits = (ids[:, None] == jnp.arange(table.shape[0], dtype=jnp.int32)[None, :]).astype(table.dtype)
    return jnp.dot(hits, table, preferred_element_type=jnp.float32).astype(table.dtype)


def attend_kernel(fetched_ref, tenc_ref, q_ref, wm_ref, wt_ref, out_ref):
    f32, bf16 = jnp.float32, jnp.bfloat16
    block = q_ref.shape[0]
    rows = fetched_ref.shape[0]
    nbrs = rows // block
    width = q_ref.shape[1]
    kv_mem = jnp.dot(fetched_ref[...], wm_ref[...], preferred_element_type=f32).astype(bf16)
    kv_time = jnp.dot(tenc_ref[...], wt_ref[...], preferred_element_type=f32)
    keyval = kv_mem.astype(f32) + kv_time
    keys = keyval[:, :width]
    values = keyval[:, width:]
    query = q_ref[...].astype(f32)
    prod = (keys.reshape(block, nbrs, width) * query[:, None, :]).reshape(rows, width)
    lane = lax.broadcasted_iota(jnp.int32, (width, 128), 0)
    col = lax.broadcasted_iota(jnp.int32, (width, 128), 1)
    head_of = (lane // HEAD_DIM == col).astype(f32)
    highest = lax.Precision.HIGHEST
    scores = jnp.dot(prod, head_of, preferred_element_type=f32, precision=highest)
    scores = (scores / math.sqrt(HEAD_DIM)).reshape(block, nbrs, 128)
    top = jnp.max(scores, axis=1, keepdims=True)
    ex = jnp.exp(scores - top)
    weights = (ex / jnp.sum(ex, axis=1, keepdims=True)).reshape(rows, 128)
    row = lax.broadcasted_iota(jnp.int32, (128, width), 0)
    lane2 = lax.broadcasted_iota(jnp.int32, (128, width), 1)
    head_to = (lane2 // HEAD_DIM == row).astype(f32)
    spread = jnp.dot(weights, head_to, preferred_element_type=f32, precision=highest)
    mixed = jnp.sum((spread * values).reshape(block, nbrs, width), axis=1)
    out_ref[...] = mixed.astype(out_ref.dtype)


def attend(fetched, time_enc, query, w_keyval_mem, w_keyval_time, block=16):
    events, width = query.shape
    nbrs = fetched.shape[0] // events
    rows = block * nbrs
    return pl.pallas_call(
        attend_kernel,
        grid=(events // block,),
        in_specs=[
            pl.BlockSpec((rows, fetched.shape[1]), lambda i: (i, 0)),
            pl.BlockSpec((rows, time_enc.shape[1]), lambda i: (i, 0)),
            pl.BlockSpec((block, width), lambda i: (i, 0)),
            pl.BlockSpec(w_keyval_mem.shape, lambda i: (0, 0)),
            pl.BlockSpec(w_keyval_time.shape, lambda i: (0, 0)),
        ],
        out_specs=pl.BlockSpec((block, width), lambda i: (i, 0)),
        out_shape=jax.ShapeDtypeStruct((events, width), jnp.bfloat16),
    )(fetched, time_enc, query, w_keyval_mem, w_keyval_time)


def on_device(
    memory,
    last_tick,
    src_local,
    dst_owner,
    dst_local,
    event_tick,
    nbr_owner,
    nbr_local,
    nbr_tick,
    freq,
    phase,
    w_message,
    gru_input,
    gru_hidden,
    gru_bias,
    w_query,
    w_keyval_mem,
    w_keyval_time,
):
    groups = lax.axis_size("nodes")
    reps = lax.axis_size("rep")
    events = src_local.shape[0]
    rows_here = memory.shape[0]
    width_m = memory.shape[1]
    neighbours = nbr_local.shape[1]
    dst_cap = max(2, 2 * events // groups)
    nbr_cap = 2 * events * neighbours // groups
    dst_slot, _, _ = place(dst_owner[:, 0], groups, dst_cap)
    nbr_slot, nbr_hot, nbr_rank = place(nbr_owner.reshape(-1), groups, nbr_cap)
    mem_half = memory.astype(jnp.bfloat16)
    near_rows = mem_half[src_local]
    near_ticks = last_tick[src_local]
    ticks = event_tick.astype(jnp.float32)

    req = jnp.stack([dst_local, event_tick, near_ticks], axis=1)
    req_ints = (
        jnp.full((groups * dst_cap, 3), -1, jnp.int32)
        .at[dst_slot]
        .set(req)
        .reshape(groups, dst_cap * 3)
    )
    nbr_ids = scatter_ids(nbr_hot, nbr_rank, nbr_local.reshape(-1), nbr_cap)
    req_rows = (
        jnp.zeros((groups * dst_cap, width_m), jnp.bfloat16)
        .at[dst_slot]
        .set(near_rows)
        .reshape(groups, dst_cap, width_m)
    )
    ints_out = jnp.concatenate([req_ints, nbr_ids], axis=1)
    ints_in = lax.all_to_all(ints_out, "nodes", split_axis=0, concat_axis=0, tiled=True)
    rows_in = lax.all_to_all(req_rows, "nodes", split_axis=0, concat_axis=0, tiled=True)
    got = ints_in[:, : dst_cap * 3].reshape(groups * dst_cap, 3)
    got_nbr = ints_in[:, dst_cap * 3 :]
    got_dst = got[:, 0]
    got_tick = got[:, 1].astype(jnp.float32)
    got_src_tick = got[:, 2].astype(jnp.float32)
    safe_dst = jnp.maximum(got_dst, 0)
    far_src = rows_in.reshape(-1, width_m)
    own_dst = mem_half[safe_dst]
    own_dst_tick = last_tick[safe_dst].astype(jnp.float32)

    src_time = encode(got_tick - got_src_tick, freq, phase).astype(jnp.bfloat16)
    dst_time = encode(got_tick - own_dst_tick, freq, phase).astype(jnp.bfloat16)
    slots = far_src.shape[0]
    stacked = jnp.concatenate(
        [
            jnp.concatenate([far_src, own_dst, src_time], axis=1),
            jnp.concatenate([own_dst, far_src, dst_time], axis=1),
        ],
        axis=0,
    )
    messages = jax.nn.silu(jnp.dot(stacked, w_message, preferred_element_type=jnp.float32)).astype(
        jnp.bfloat16
    )
    msg_src_slots = messages[:slots]
    msg_dst = messages[slots:]
    back = lax.all_to_all(
        msg_src_slots.reshape(groups, dst_cap, -1), "nodes", split_axis=0, concat_axis=0, tiled=True
    )
    msg_src = back.reshape(-1, back.shape[2])[dst_slot]

    def spread(value):
        parts = [value]
        for shift in range(1, reps):
            pairs = [(i, (i + shift) % reps) for i in range(reps)]
            parts.append(lax.ppermute(value, "rep", pairs))
        return parts

    local_ids = jnp.concatenate([got_dst, src_local], axis=0)
    id_hi, id_lo = split_pairs(local_ids + 1)
    id_rows = -(-2 * local_ids.shape[0] // width_m)
    id_rows = -(-id_rows // 16) * 16
    id_block = jnp.concatenate(
        [id_hi, id_lo, jnp.zeros((id_rows * width_m - 2 * local_ids.shape[0],), jnp.bfloat16)]
    ).reshape(id_rows, width_m)
    early = spread(jnp.concatenate([msg_dst, id_block], axis=0))
    late = spread(msg_src)
    count = msg_dst.shape[0]
    total = local_ids.shape[0]
    all_msgs = jnp.concatenate([p[:count] for p in early] + late, axis=0)
    coded = jnp.stack([p[count:].reshape(-1)[: 2 * total] for p in early]).astype(jnp.int32)
    ids = coded[:, :total] * 32 + coded[:, total:] - 1
    all_ids = jnp.concatenate([ids[:, :count].reshape(-1), ids[:, count:].reshape(-1)])
    row_ids = jnp.arange(rows_here, dtype=jnp.int32)[:, None]
    hits = row_ids == all_ids[None, :]
    sums = jnp.dot(hits.astype(jnp.bfloat16), all_msgs, preferred_element_type=jnp.float32)
    counts = jnp.sum(hits.astype(jnp.float32), axis=1)

    unit_width = gru_bias.shape[1]
    start = lax.axis_index("rep") * unit_width
    state_part = lax.dynamic_slice_in_dim(memory, start, unit_width, 1)
    mean = sums / jnp.maximum(counts, 1.0)[:, None]
    highest = lax.Precision.HIGHEST
    a_parts = jnp.einsum("rk,gku->gru", mean, gru_input, precision=highest)
    b_parts = jnp.einsum("rk,gku->gru", memory, gru_hidden, precision=highest)
    update = jax.nn.sigmoid(a_parts[0] + b_parts[0] + gru_bias[0])
    reset = jax.nn.sigmoid(a_parts[1] + b_parts[1] + gru_bias[1])
    cand = jnp.tanh(a_parts[2] + gru_bias[2] + reset * (b_parts[2] + gru_bias[3]))
    fresh = (1.0 - update) * cand + update * state_part
    new_part = jnp.where((counts > 0.0)[:, None], fresh, state_part)
    updated = lax.all_gather(new_part.astype(jnp.bfloat16), "rep", axis=1, tiled=True)
    served = select_rows(got_nbr.reshape(-1), updated).reshape(groups, nbr_cap, -1)
    returned = lax.all_to_all(served, "nodes", split_axis=0, concat_axis=0, tiled=True)
    fetched = returned.reshape(-1, updated.shape[1])[nbr_slot]
    gaps = ticks[:, None] - nbr_tick.astype(jnp.float32)
    time_enc = encode(gaps, freq, phase).reshape(-1, freq.shape[0]).astype(jnp.bfloat16)
    query = jnp.dot(updated[src_local], w_query, preferred_element_type=jnp.float32).astype(
        jnp.bfloat16
    )
    embed = attend(fetched, time_enc, query, w_keyval_mem, w_keyval_time)
    return (new_part, embed)


def solution(mesh):
    placed = (
        P("nodes", None),
        P("nodes"),
        P(("nodes", "rep")),
        P(("nodes", "rep"), None),
        P(("nodes", "rep")),
        P(("nodes", "rep")),
        P(("nodes", "rep"), None, None),
        P(("nodes", "rep"), None),
        P(("nodes", "rep"), None),
        P(),
        P(),
        P(),
        P(None, None, "rep"),
        P(None, None, "rep"),
        P(None, "rep"),
        P(),
        P(),
        P(),
    )
    return jax.shard_map(
        on_device,
        mesh=mesh,
        in_specs=placed,
        out_specs=(P("nodes", "rep"), P(("nodes", "rep"), None)),
        check_vma=False,
    )
```

```python
import math

import jax
import jax.numpy as jnp
from jax import lax
from jax.experimental import pallas as pl
from jax.sharding import PartitionSpec as P


HEAD_DIM = 64


def encode(gaps, freq, phase):
    return jnp.cos(gaps[..., None] * freq + phase)


def place(owner, groups, capacity):
    onehot = (owner[:, None] == jnp.arange(groups, dtype=jnp.int32)[None, :]).astype(jnp.int32)
    before = jnp.cumsum(onehot, axis=0) - onehot
    rank = jnp.sum(before * onehot, axis=1)
    return owner * capacity + rank, onehot, rank


def split_pairs(v):
    return (v // 32).astype(jnp.bfloat16), (v % 32).astype(jnp.bfloat16)


def scatter_ids(onehot, rank, values, capacity):
    hi, lo = split_pairs(values + 1)
    at_rank = rank[:, None] == jnp.arange(capacity, dtype=jnp.int32)[None, :]
    cols = jnp.concatenate(
        [jnp.where(at_rank, hi[:, None], 0.0), jnp.where(at_rank, lo[:, None], 0.0)], axis=1
    ).astype(jnp.bfloat16)
    table = jnp.dot(onehot.T.astype(jnp.bfloat16), cols, preferred_element_type=jnp.float32)
    table = table.astype(jnp.int32)
    return table[:, :capacity] * 32 + table[:, capacity:] - 1


def select_rows(ids, table):
    hits = (ids[:, None] == jnp.arange(table.shape[0], dtype=jnp.int32)[None, :]).astype(table.dtype)
    return jnp.dot(hits, table, preferred_element_type=jnp.float32).astype(table.dtype)


def attend_kernel(fetched_ref, tenc_ref, q_ref, wm_ref, wt_ref, out_ref):
    f32, bf16 = jnp.float32, jnp.bfloat16
    block = q_ref.shape[0]
    rows = fetched_ref.shape[0]
    nbrs = rows // block
    width = q_ref.shape[1]
    kv_mem = jnp.dot(fetched_ref[...], wm_ref[...], preferred_element_type=f32).astype(bf16)
    kv_time = jnp.dot(tenc_ref[...], wt_ref[...], preferred_element_type=f32)
    keyval = kv_mem.astype(f32) + kv_time
    keys = keyval[:, :width]
    values = keyval[:, width:]
    query = q_ref[...].astype(f32)
    prod = (keys.reshape(block, nbrs, width) * query[:, None, :]).reshape(rows, width)
    lane = lax.broadcasted_iota(jnp.int32, (width, 128), 0)
    col = lax.broadcasted_iota(jnp.int32, (width, 128), 1)
    head_of = (lane // HEAD_DIM == col).astype(f32)
    highest = lax.Precision.HIGHEST
    scores = jnp.dot(prod, head_of, preferred_element_type=f32, precision=highest)
    scores = (scores / math.sqrt(HEAD_DIM)).reshape(block, nbrs, 128)
    top = jnp.max(scores, axis=1, keepdims=True)
    ex = jnp.exp(scores - top)
    weights = (ex / jnp.sum(ex, axis=1, keepdims=True)).reshape(rows, 128)
    row = lax.broadcasted_iota(jnp.int32, (128, width), 0)
    lane2 = lax.broadcasted_iota(jnp.int32, (128, width), 1)
    head_to = (lane2 // HEAD_DIM == row).astype(f32)
    spread = jnp.dot(weights, head_to, preferred_element_type=f32, precision=highest)
    mixed = jnp.sum((spread * values).reshape(block, nbrs, width), axis=1)
    out_ref[...] = mixed.astype(out_ref.dtype)


def attend(fetched, time_enc, query, w_keyval_mem, w_keyval_time, block=16):
    events, width = query.shape
    nbrs = fetched.shape[0] // events
    rows = block * nbrs
    return pl.pallas_call(
        attend_kernel,
        grid=(events // block,),
        in_specs=[
            pl.BlockSpec((rows, fetched.shape[1]), lambda i: (i, 0)),
            pl.BlockSpec((rows, time_enc.shape[1]), lambda i: (i, 0)),
            pl.BlockSpec((block, width), lambda i: (i, 0)),
            pl.BlockSpec(w_keyval_mem.shape, lambda i: (0, 0)),
            pl.BlockSpec(w_keyval_time.shape, lambda i: (0, 0)),
        ],
        out_specs=pl.BlockSpec((block, width), lambda i: (i, 0)),
        out_shape=jax.ShapeDtypeStruct((events, width), jnp.bfloat16),
    )(fetched, time_enc, query, w_keyval_mem, w_keyval_time)


def on_device_body(
    memory,
    last_tick,
    src_local,
    dst_owner,
    dst_local,
    event_tick,
    nbr_owner,
    nbr_local,
    nbr_tick,
    freq,
    phase,
    w_message,
    gru_input,
    gru_hidden,
    gru_bias,
    w_query,
    w_keyval_mem,
    w_keyval_time,
):
    groups = lax.axis_size("nodes")
    reps = lax.axis_size("rep")
    events = src_local.shape[0]
    rows_here = memory.shape[0]
    width_m = memory.shape[1]
    neighbours = nbr_local.shape[1]
    dst_cap = max(2, 2 * events // groups)
    nbr_cap = 2 * events * neighbours // groups
    dst_slot, _, _ = place(dst_owner[:, 0], groups, dst_cap)
    nbr_slot, nbr_hot, nbr_rank = place(nbr_owner.reshape(-1), groups, nbr_cap)
    mem_half = memory.astype(jnp.bfloat16)
    near_rows = mem_half[src_local]
    near_ticks = last_tick[src_local]
    ticks = event_tick.astype(jnp.float32)

    req = jnp.stack([dst_local, event_tick, near_ticks], axis=1)
    req_ints = (
        jnp.full((groups * dst_cap, 3), -1, jnp.int32)
        .at[dst_slot]
        .set(req)
        .reshape(groups, dst_cap * 3)
    )
    nbr_ids = scatter_ids(nbr_hot, nbr_rank, nbr_local.reshape(-1), nbr_cap)
    req_rows = (
        jnp.zeros((groups * dst_cap, width_m), jnp.bfloat16)
        .at[dst_slot]
        .set(near_rows)
        .reshape(groups, dst_cap, width_m)
    )
    ints_out = jnp.concatenate([req_ints, nbr_ids], axis=1)
    ints_in = lax.all_to_all(ints_out, "nodes", split_axis=0, concat_axis=0, tiled=True)
    rows_in = lax.all_to_all(req_rows, "nodes", split_axis=0, concat_axis=0, tiled=True)
    got = ints_in[:, : dst_cap * 3].reshape(groups * dst_cap, 3)
    got_nbr = ints_in[:, dst_cap * 3 :]
    got_dst = got[:, 0]
    got_tick = got[:, 1].astype(jnp.float32)
    got_src_tick = got[:, 2].astype(jnp.float32)
    safe_dst = jnp.maximum(got_dst, 0)
    far_src = rows_in.reshape(-1, width_m)
    own_dst = mem_half[safe_dst]
    own_dst_tick = last_tick[safe_dst].astype(jnp.float32)

    src_time = encode(got_tick - got_src_tick, freq, phase).astype(jnp.bfloat16)
    dst_time = encode(got_tick - own_dst_tick, freq, phase).astype(jnp.bfloat16)
    slots = far_src.shape[0]
    stacked = jnp.concatenate(
        [
            jnp.concatenate([far_src, own_dst, src_time], axis=1),
            jnp.concatenate([own_dst, far_src, dst_time], axis=1),
        ],
        axis=0,
    )
    messages = jax.nn.silu(jnp.dot(stacked, w_message, preferred_element_type=jnp.float32)).astype(
        jnp.bfloat16
    )
    msg_src_slots = messages[:slots]
    msg_dst = messages[slots:]
    back = lax.all_to_all(
        msg_src_slots.reshape(groups, dst_cap, -1), "nodes", split_axis=0, concat_axis=0, tiled=True
    )
    msg_src = back.reshape(-1, back.shape[2])[dst_slot]

    def spread(value):
        parts = [value]
        for shift in range(1, reps):
            pairs = [(i, (i + shift) % reps) for i in range(reps)]
            parts.append(lax.ppermute(value, "rep", pairs))
        return parts

    local_ids = jnp.concatenate([got_dst, src_local], axis=0)
    id_hi, id_lo = split_pairs(local_ids + 1)
    id_rows = -(-2 * local_ids.shape[0] // width_m)
    id_rows = -(-id_rows // 16) * 16
    id_block = jnp.concatenate(
        [id_hi, id_lo, jnp.zeros((id_rows * width_m - 2 * local_ids.shape[0],), jnp.bfloat16)]
    ).reshape(id_rows, width_m)
    early = spread(jnp.concatenate([msg_dst, id_block], axis=0))
    late = spread(msg_src)
    count = msg_dst.shape[0]
    total = local_ids.shape[0]
    all_msgs = jnp.concatenate([p[:count] for p in early] + late, axis=0)
    coded = jnp.stack([p[count:].reshape(-1)[: 2 * total] for p in early]).astype(jnp.int32)
    ids = coded[:, :total] * 32 + coded[:, total:] - 1
    all_ids = jnp.concatenate([ids[:, :count].reshape(-1), ids[:, count:].reshape(-1)])
    row_ids = jnp.arange(rows_here, dtype=jnp.int32)[:, None]
    hits = row_ids == all_ids[None, :]
    sums = jnp.dot(hits.astype(jnp.bfloat16), all_msgs, preferred_element_type=jnp.float32)
    counts = jnp.sum(hits.astype(jnp.float32), axis=1)

    unit_width = gru_bias.shape[1]
    start = lax.axis_index("rep") * unit_width
    state_part = lax.dynamic_slice_in_dim(memory, start, unit_width, 1)
    mean = sums / jnp.maximum(counts, 1.0)[:, None]
    highest = lax.Precision.HIGHEST
    a_parts = jnp.einsum("rk,gku->gru", mean, gru_input, precision=highest)
    b_parts = jnp.einsum("rk,gku->gru", memory, gru_hidden, precision=highest)
    update = jax.nn.sigmoid(a_parts[0] + b_parts[0] + gru_bias[0])
    reset = jax.nn.sigmoid(a_parts[1] + b_parts[1] + gru_bias[1])
    cand = jnp.tanh(a_parts[2] + gru_bias[2] + reset * (b_parts[2] + gru_bias[3]))
    fresh = (1.0 - update) * cand + update * state_part
    new_part = jnp.where((counts > 0.0)[:, None], fresh, state_part)
    updated = lax.all_gather(new_part.astype(jnp.bfloat16), "rep", axis=1, tiled=True)
    served = select_rows(got_nbr.reshape(-1), updated).reshape(groups, nbr_cap, -1)
    returned = lax.all_to_all(served, "nodes", split_axis=0, concat_axis=0, tiled=True)
    fetched = returned.reshape(-1, updated.shape[1])[nbr_slot]
    gaps = ticks[:, None] - nbr_tick.astype(jnp.float32)
    time_enc = encode(gaps, freq, phase).reshape(-1, freq.shape[0]).astype(jnp.bfloat16)
    query = jnp.dot(updated[src_local], w_query, preferred_element_type=jnp.float32).astype(
        jnp.bfloat16
    )
    embed = attend(fetched, time_enc, query, w_keyval_mem, w_keyval_time)
    return (new_part, embed)


def solution(mesh):
    placed = (
        P("nodes", None),
        P("nodes"),
        P(("nodes", "rep")),
        P(("nodes", "rep"), None),
        P(("nodes", "rep")),
        P(("nodes", "rep")),
        P(("nodes", "rep"), None, None),
        P(("nodes", "rep"), None),
        P(("nodes", "rep"), None),
        P(),
        P(),
        P(),
        P(None, None, "rep"),
        P(None, None, "rep"),
        P(None, "rep"),
        P(),
        P(),
        P(),
    )
    return jax.shard_map(
        on_device_body,
        mesh=mesh,
        in_specs=placed,
        out_specs=(P("nodes", "rep"), P(("nodes", "rep"), None)),
        check_vma=False,
    )
```

```python
import math

import jax
import jax.numpy as jnp
from jax import lax
from jax.experimental import pallas as pl
from jax.experimental.pallas import tpu as pltpu
from jax.sharding import PartitionSpec as P

HEADS = 8
HEAD_DIM = 64


def encode(gaps, freq, phase):
    return jnp.cos(gaps[..., None] * freq + phase)


def place(owner, groups, capacity):
    onehot = (owner[:, None] == jnp.arange(groups, dtype=jnp.int32)[None, :]).astype(jnp.int32)
    before = jnp.cumsum(onehot, axis=0) - onehot
    rank = jnp.sum(before * onehot, axis=1)
    return owner * capacity + rank, onehot, rank


def split_pairs(v):
    return (v // 32).astype(jnp.bfloat16), (v % 32).astype(jnp.bfloat16)


def scatter_ids(onehot, rank, values, capacity):
    hi, lo = split_pairs(values + 1)
    at_rank = rank[:, None] == jnp.arange(capacity, dtype=jnp.int32)[None, :]
    cols = jnp.concatenate(
        [jnp.where(at_rank, hi[:, None], 0.0), jnp.where(at_rank, lo[:, None], 0.0)], axis=1
    ).astype(jnp.bfloat16)
    table = jnp.dot(onehot.T.astype(jnp.bfloat16), cols, preferred_element_type=jnp.float32)
    table = table.astype(jnp.int32)
    return table[:, :capacity] * 32 + table[:, capacity:] - 1


def select_rows(ids, table):
    hits = (ids[:, None] == jnp.arange(table.shape[0], dtype=jnp.int32)[None, :]).astype(table.dtype)
    return jnp.dot(hits, table, preferred_element_type=jnp.float32).astype(table.dtype)


def attend_kernel(fetched_ref, tenc_ref, q_ref, wm_ref, wt_ref, out_ref):
    f32, bf16 = jnp.float32, jnp.bfloat16
    block = q_ref.shape[0]
    rows = fetched_ref.shape[0]
    nbrs = rows // block
    width = q_ref.shape[1]
    kv_mem = jnp.dot(fetched_ref[...], wm_ref[...], preferred_element_type=f32).astype(bf16)
    kv_time = jnp.dot(tenc_ref[...], wt_ref[...], preferred_element_type=f32)
    keyval = kv_mem.astype(f32) + kv_time
    keys = keyval[:, :width]
    values = keyval[:, width:]
    query = q_ref[...].astype(f32)
    prod = (keys.reshape(block, nbrs, width) * query[:, None, :]).reshape(rows, width)
    lane = lax.broadcasted_iota(jnp.int32, (width, 128), 0)
    col = lax.broadcasted_iota(jnp.int32, (width, 128), 1)
    head_of = (lane // HEAD_DIM == col).astype(f32)
    highest = lax.Precision.HIGHEST
    scores = jnp.dot(prod, head_of, preferred_element_type=f32, precision=highest)
    scores = (scores / math.sqrt(HEAD_DIM)).reshape(block, nbrs, 128)
    top = jnp.max(scores, axis=1, keepdims=True)
    ex = jnp.exp(scores - top)
    weights = (ex / jnp.sum(ex, axis=1, keepdims=True)).reshape(rows, 128)
    row = lax.broadcasted_iota(jnp.int32, (128, width), 0)
    lane2 = lax.broadcasted_iota(jnp.int32, (128, width), 1)
    head_to = (lane2 // HEAD_DIM == row).astype(f32)
    spread = jnp.dot(weights, head_to, preferred_element_type=f32, precision=highest)
    mixed = jnp.sum((spread * values).reshape(block, nbrs, width), axis=1)
    out_ref[...] = mixed.astype(out_ref.dtype)


def attend(fetched, time_enc, query, w_keyval_mem, w_keyval_time, block=16):
    events, width = query.shape
    nbrs = fetched.shape[0] // events
    rows = block * nbrs
    return pl.pallas_call(
        attend_kernel,
        grid=(events // block,),
        in_specs=[
            pl.BlockSpec((rows, fetched.shape[1]), lambda i: (i, 0)),
            pl.BlockSpec((rows, time_enc.shape[1]), lambda i: (i, 0)),
            pl.BlockSpec((block, width), lambda i: (i, 0)),
            pl.BlockSpec(w_keyval_mem.shape, lambda i: (0, 0)),
            pl.BlockSpec(w_keyval_time.shape, lambda i: (0, 0)),
        ],
        out_specs=pl.BlockSpec((block, width), lambda i: (i, 0)),
        out_shape=jax.ShapeDtypeStruct((events, width), jnp.bfloat16),
    )(fetched, time_enc, query, w_keyval_mem, w_keyval_time)


def on_device(
    memory,
    last_tick,
    src_local,
    dst_owner,
    dst_local,
    event_tick,
    nbr_owner,
    nbr_local,
    nbr_tick,
    freq,
    phase,
    w_message,
    gru_input,
    gru_hidden,
    gru_bias,
    w_query,
    w_keyval_mem,
    w_keyval_time,
):
    groups = lax.axis_size("nodes")
    reps = lax.axis_size("rep")
    events = src_local.shape[0]
    rows_here = memory.shape[0]
    width_m = memory.shape[1]
    neighbours = nbr_local.shape[1]
    dst_cap = max(2, 2 * events // groups)
    nbr_cap = 2 * events * neighbours // groups
    dst_slot, _, _ = place(dst_owner[:, 0], groups, dst_cap)
    nbr_slot, nbr_hot, nbr_rank = place(nbr_owner.reshape(-1), groups, nbr_cap)
    mem_half = memory.astype(jnp.bfloat16)
    near_rows = mem_half[src_local]
    near_ticks = last_tick[src_local]
    ticks = event_tick.astype(jnp.float32)

    req = jnp.stack([dst_local, event_tick, near_ticks], axis=1)
    req_ints = (
        jnp.full((groups * dst_cap, 3), -1, jnp.int32)
        .at[dst_slot]
        .set(req)
        .reshape(groups, dst_cap * 3)
    )
    nbr_ids = scatter_ids(nbr_hot, nbr_rank, nbr_local.reshape(-1), nbr_cap)
    req_rows = (
        jnp.zeros((groups * dst_cap, width_m), jnp.bfloat16)
        .at[dst_slot]
        .set(near_rows)
        .reshape(groups, dst_cap, width_m)
    )
    ints_out = jnp.concatenate([req_ints, nbr_ids], axis=1)
    ints_in = lax.all_to_all(ints_out, "nodes", split_axis=0, concat_axis=0, tiled=True)
    rows_in = lax.all_to_all(req_rows, "nodes", split_axis=0, concat_axis=0, tiled=True)
    got = ints_in[:, : dst_cap * 3].reshape(groups * dst_cap, 3)
    got_nbr = ints_in[:, dst_cap * 3 :]
    got_dst = got[:, 0]
    got_tick = got[:, 1].astype(jnp.float32)
    got_src_tick = got[:, 2].astype(jnp.float32)
    safe_dst = jnp.maximum(got_dst, 0)
    far_src = rows_in.reshape(-1, width_m)
    own_dst = mem_half[safe_dst]
    own_dst_tick = last_tick[safe_dst].astype(jnp.float32)

    src_time = encode(got_tick - got_src_tick, freq, phase).astype(jnp.bfloat16)
    dst_time = encode(got_tick - own_dst_tick, freq, phase).astype(jnp.bfloat16)
    slots = far_src.shape[0]
    stacked = jnp.concatenate(
        [
            jnp.concatenate([far_src, own_dst, src_time], axis=1),
            jnp.concatenate([own_dst, far_src, dst_time], axis=1),
        ],
        axis=0,
    )
    messages = jax.nn.silu(jnp.dot(stacked, w_message, preferred_element_type=jnp.float32)).astype(
        jnp.bfloat16
    )
    msg_src_slots = messages[:slots]
    msg_dst = messages[slots:]
    back = lax.all_to_all(
        msg_src_slots.reshape(groups, dst_cap, -1), "nodes", split_axis=0, concat_axis=0, tiled=True
    )
    msg_src = back.reshape(-1, back.shape[2])[dst_slot]

    local_msgs = jnp.concatenate([msg_src, msg_dst], axis=0)
    local_ids = jnp.concatenate([src_local, got_dst], axis=0)
    id_hi, id_lo = split_pairs(local_ids + 1)
    id_rows = -(-2 * local_ids.shape[0] // width_m)
    id_rows = -(-id_rows // 16) * 16
    id_block = jnp.concatenate(
        [id_hi, id_lo, jnp.zeros((id_rows * width_m - 2 * local_ids.shape[0],), jnp.bfloat16)]
    ).reshape(id_rows, width_m)
    payload = jnp.concatenate([local_msgs, id_block], axis=0)
    gathered = lax.all_gather(payload, "rep", axis=0, tiled=True).reshape(reps, *payload.shape)
    parts = [gathered[r] for r in range(reps)]
    count = local_msgs.shape[0]
    all_msgs = jnp.concatenate([p[:count] for p in parts], axis=0)
    coded = jnp.stack([p[count:].reshape(-1)[: 2 * count] for p in parts]).astype(jnp.int32)
    all_ids = (coded[:, :count] * 32 + coded[:, count:] - 1).reshape(-1)
    row_ids = jnp.arange(rows_here, dtype=jnp.int32)[:, None]
    hits = row_ids == all_ids[None, :]
    sums = jnp.dot(hits.astype(jnp.bfloat16), all_msgs, preferred_element_type=jnp.float32)
    counts = jnp.sum(hits.astype(jnp.float32), axis=1)

    unit_width = gru_bias.shape[1]
    start = lax.axis_index("rep") * unit_width
    state_part = lax.dynamic_slice_in_dim(memory, start, unit_width, 1)
    mean = sums / jnp.maximum(counts, 1.0)[:, None]
    highest = lax.Precision.HIGHEST
    a_parts = jnp.einsum("rk,gku->gru", mean, gru_input, precision=highest)
    b_parts = jnp.einsum("rk,gku->gru", memory, gru_hidden, precision=highest)
    update = jax.nn.sigmoid(a_parts[0] + b_parts[0] + gru_bias[0])
    reset = jax.nn.sigmoid(a_parts[1] + b_parts[1] + gru_bias[1])
    cand = jnp.tanh(a_parts[2] + gru_bias[2] + reset * (b_parts[2] + gru_bias[3]))
    fresh = (1.0 - update) * cand + update * state_part
    new_part = jnp.where((counts > 0.0)[:, None], fresh, state_part)
    updated = lax.all_gather(new_part.astype(jnp.bfloat16), "rep", axis=1, tiled=True)
    served = select_rows(got_nbr.reshape(-1), updated).reshape(groups, nbr_cap, -1)
    returned = lax.all_to_all(served, "nodes", split_axis=0, concat_axis=0, tiled=True)
    fetched = returned.reshape(-1, updated.shape[1])[nbr_slot]
    gaps = ticks[:, None] - nbr_tick.astype(jnp.float32)
    time_enc = encode(gaps, freq, phase).reshape(-1, freq.shape[0]).astype(jnp.bfloat16)
    query = jnp.dot(updated[src_local], w_query, preferred_element_type=jnp.float32).astype(
        jnp.bfloat16
    )
    embed = attend(fetched, time_enc, query, w_keyval_mem, w_keyval_time)
    return (new_part, embed)


def solution(mesh):
    placed = (
        P("nodes", None),
        P("nodes"),
        P(("nodes", "rep")),
        P(("nodes", "rep"), None),
        P(("nodes", "rep")),
        P(("nodes", "rep")),
        P(("nodes", "rep"), None, None),
        P(("nodes", "rep"), None),
        P(("nodes", "rep"), None),
        P(),
        P(),
        P(),
        P(None, None, "rep"),
        P(None, None, "rep"),
        P(None, "rep"),
        P(),
        P(),
        P(),
    )
    return jax.shard_map(
        on_device,
        mesh=mesh,
        in_specs=placed,
        out_specs=(P("nodes", "rep"), P(("nodes", "rep"), None)),
        check_vma=False,
    )
```

```python
import math

import jax
import jax.numpy as jnp
from jax import lax
from jax.experimental import pallas as pl
from jax.experimental.pallas import tpu as pltpu
from jax.sharding import PartitionSpec as P

HEADS = 8
HEAD_DIM = 64


def encode(gaps, freq, phase):
    return jnp.cos(gaps[..., None] * freq + phase)


def place(owner, groups, capacity):
    onehot = (owner[:, None] == jnp.arange(groups, dtype=jnp.int32)[None, :]).astype(jnp.int32)
    before = jnp.cumsum(onehot, axis=0) - onehot
    rank = jnp.sum(before * onehot, axis=1)
    return owner * capacity + rank, onehot, rank


def split_pairs(v):
    return (v // 32).astype(jnp.bfloat16), (v % 32).astype(jnp.bfloat16)


def scatter_ids(onehot, rank, values, capacity):
    hi, lo = split_pairs(values + 1)
    at_rank = rank[:, None] == jnp.arange(capacity, dtype=jnp.int32)[None, :]
    cols = jnp.concatenate(
        [jnp.where(at_rank, hi[:, None], 0.0), jnp.where(at_rank, lo[:, None], 0.0)], axis=1
    ).astype(jnp.bfloat16)
    table = jnp.dot(onehot.T.astype(jnp.bfloat16), cols, preferred_element_type=jnp.float32)
    table = table.astype(jnp.int32)
    return table[:, :capacity] * 32 + table[:, capacity:] - 1


def select_rows(ids, table):
    hits = (ids[:, None] == jnp.arange(table.shape[0], dtype=jnp.int32)[None, :]).astype(table.dtype)
    return jnp.dot(hits, table, preferred_element_type=jnp.float32).astype(table.dtype)


def attend_kernel(fetched_ref, tenc_ref, q_ref, wm_ref, wt_ref, out_ref):
    f32, bf16 = jnp.float32, jnp.bfloat16
    block = q_ref.shape[0]
    rows = fetched_ref.shape[0]
    nbrs = rows // block
    width = q_ref.shape[1]
    kv_mem = jnp.dot(fetched_ref[...], wm_ref[...], preferred_element_type=f32).astype(bf16)
    kv_time = jnp.dot(tenc_ref[...], wt_ref[...], preferred_element_type=f32)
    keyval = kv_mem.astype(f32) + kv_time
    keys = keyval[:, :width]
    values = keyval[:, width:]
    query = q_ref[...].astype(f32)
    prod = (keys.reshape(block, nbrs, width) * query[:, None, :]).reshape(rows, width)
    lane = lax.broadcasted_iota(jnp.int32, (width, 128), 0)
    col = lax.broadcasted_iota(jnp.int32, (width, 128), 1)
    head_of = (lane // HEAD_DIM == col).astype(bf16)
    hi = prod.astype(bf16)
    lo = (prod - hi.astype(f32)).astype(bf16)
    scores = jnp.dot(hi, head_of, preferred_element_type=f32) + jnp.dot(
        lo, head_of, preferred_element_type=f32
    )
    scores = (scores / math.sqrt(HEAD_DIM)).reshape(block, nbrs, 128)
    top = jnp.max(scores, axis=1, keepdims=True)
    ex = jnp.exp(scores - top)
    weights = (ex / jnp.sum(ex, axis=1, keepdims=True)).reshape(rows, 128)
    row = lax.broadcasted_iota(jnp.int32, (128, width), 0)
    lane2 = lax.broadcasted_iota(jnp.int32, (128, width), 1)
    head_to = (lane2 // HEAD_DIM == row).astype(bf16)
    w_hi = weights.astype(bf16)
    w_lo = (weights - w_hi.astype(f32)).astype(bf16)
    spread = jnp.dot(w_hi, head_to, preferred_element_type=f32) + jnp.dot(
        w_lo, head_to, preferred_element_type=f32
    )
    mixed = jnp.sum((spread * values).reshape(block, nbrs, width), axis=1)
    out_ref[...] = mixed.astype(out_ref.dtype)


def attend(fetched, time_enc, query, w_keyval_mem, w_keyval_time, block=32):
    events, width = query.shape
    nbrs = fetched.shape[0] // events
    rows = block * nbrs
    return pl.pallas_call(
        attend_kernel,
        grid=(events // block,),
        in_specs=[
            pl.BlockSpec((rows, fetched.shape[1]), lambda i: (i, 0)),
            pl.BlockSpec((rows, time_enc.shape[1]), lambda i: (i, 0)),
            pl.BlockSpec((block, width), lambda i: (i, 0)),
            pl.BlockSpec(w_keyval_mem.shape, lambda i: (0, 0)),
            pl.BlockSpec(w_keyval_time.shape, lambda i: (0, 0)),
        ],
        out_specs=pl.BlockSpec((block, width), lambda i: (i, 0)),
        out_shape=jax.ShapeDtypeStruct((events, width), jnp.bfloat16),
    )(fetched, time_enc, query, w_keyval_mem, w_keyval_time)


def on_device(
    memory,
    last_tick,
    src_local,
    dst_owner,
    dst_local,
    event_tick,
    nbr_owner,
    nbr_local,
    nbr_tick,
    freq,
    phase,
    w_message,
    gru_input,
    gru_hidden,
    gru_bias,
    w_query,
    w_keyval_mem,
    w_keyval_time,
):
    groups = lax.axis_size("nodes")
    reps = lax.axis_size("rep")
    events = src_local.shape[0]
    rows_here = memory.shape[0]
    width_m = memory.shape[1]
    neighbours = nbr_local.shape[1]
    dst_cap = max(2, 2 * events // groups)
    nbr_cap = 2 * events * neighbours // groups
    dst_slot, _, _ = place(dst_owner[:, 0], groups, dst_cap)
    nbr_slot, nbr_hot, nbr_rank = place(nbr_owner.reshape(-1), groups, nbr_cap)
    mem_half = memory.astype(jnp.bfloat16)
    near_rows = mem_half[src_local]
    near_ticks = last_tick[src_local]
    ticks = event_tick.astype(jnp.float32)

    req = jnp.stack([dst_local, event_tick, near_ticks], axis=1)
    req_ints = (
        jnp.full((groups * dst_cap, 3), -1, jnp.int32)
        .at[dst_slot]
        .set(req)
        .reshape(groups, dst_cap * 3)
    )
    nbr_ids = scatter_ids(nbr_hot, nbr_rank, nbr_local.reshape(-1), nbr_cap)
    req_rows = (
        jnp.zeros((groups * dst_cap, width_m), jnp.bfloat16)
        .at[dst_slot]
        .set(near_rows)
        .reshape(groups, dst_cap, width_m)
    )
    ints_out = jnp.concatenate([req_ints, nbr_ids], axis=1)
    ints_in = lax.all_to_all(ints_out, "nodes", split_axis=0, concat_axis=0, tiled=True)
    rows_in = lax.all_to_all(req_rows, "nodes", split_axis=0, concat_axis=0, tiled=True)
    got = ints_in[:, : dst_cap * 3].reshape(groups * dst_cap, 3)
    got_nbr = ints_in[:, dst_cap * 3 :]
    got_dst = got[:, 0]
    got_tick = got[:, 1].astype(jnp.float32)
    got_src_tick = got[:, 2].astype(jnp.float32)
    safe_dst = jnp.maximum(got_dst, 0)
    far_src = rows_in.reshape(-1, width_m)
    own_dst = mem_half[safe_dst]
    own_dst_tick = last_tick[safe_dst].astype(jnp.float32)

    src_time = encode(got_tick - got_src_tick, freq, phase).astype(jnp.bfloat16)
    dst_time = encode(got_tick - own_dst_tick, freq, phase).astype(jnp.bfloat16)
    slots = far_src.shape[0]
    stacked = jnp.concatenate(
        [
            jnp.concatenate([far_src, own_dst, src_time], axis=1),
            jnp.concatenate([own_dst, far_src, dst_time], axis=1),
        ],
        axis=0,
    )
    messages = jax.nn.silu(jnp.dot(stacked, w_message, preferred_element_type=jnp.float32)).astype(
        jnp.bfloat16
    )
    msg_src_slots = messages[:slots]
    msg_dst = messages[slots:]
    back = lax.all_to_all(
        msg_src_slots.reshape(groups, dst_cap, -1), "nodes", split_axis=0, concat_axis=0, tiled=True
    )
    msg_src = back.reshape(-1, back.shape[2])[dst_slot]

    local_msgs = jnp.concatenate([msg_src, msg_dst], axis=0)
    local_ids = jnp.concatenate([src_local, got_dst], axis=0)
    id_hi, id_lo = split_pairs(local_ids + 1)
    id_rows = -(-2 * local_ids.shape[0] // width_m)
    id_rows = -(-id_rows // 16) * 16
    id_block = jnp.concatenate(
        [id_hi, id_lo, jnp.zeros((id_rows * width_m - 2 * local_ids.shape[0],), jnp.bfloat16)]
    ).reshape(id_rows, width_m)
    payload = jnp.concatenate([local_msgs, id_block], axis=0)
    parts = [payload]
    for shift in range(1, reps):
        pairs = [(i, (i + shift) % reps) for i in range(reps)]
        parts.append(lax.ppermute(payload, "rep", pairs))
    count = local_msgs.shape[0]
    all_msgs = jnp.concatenate([p[:count] for p in parts], axis=0)
    coded = jnp.stack([p[count:].reshape(-1)[: 2 * count] for p in parts]).astype(jnp.int32)
    all_ids = (coded[:, :count] * 32 + coded[:, count:] - 1).reshape(-1)
    row_ids = jnp.arange(rows_here, dtype=jnp.int32)[:, None]
    hits = row_ids == all_ids[None, :]
    sums = jnp.dot(hits.astype(jnp.bfloat16), all_msgs, preferred_element_type=jnp.float32)
    counts = jnp.sum(hits.astype(jnp.float32), axis=1)

    unit_width = gru_bias.shape[1]
    start = lax.axis_index("rep") * unit_width
    state_part = lax.dynamic_slice_in_dim(memory, start, unit_width, 1)
    mean = sums / jnp.maximum(counts, 1.0)[:, None]
    highest = lax.Precision.HIGHEST
    a_parts = jnp.einsum("rk,gku->gru", mean, gru_input, precision=highest)
    b_parts = jnp.einsum("rk,gku->gru", memory, gru_hidden, precision=highest)
    update = jax.nn.sigmoid(a_parts[0] + b_parts[0] + gru_bias[0])
    reset = jax.nn.sigmoid(a_parts[1] + b_parts[1] + gru_bias[1])
    cand = jnp.tanh(a_parts[2] + gru_bias[2] + reset * (b_parts[2] + gru_bias[3]))
    fresh = (1.0 - update) * cand + update * state_part
    new_part = jnp.where((counts > 0.0)[:, None], fresh, state_part)
    updated = lax.all_gather(new_part.astype(jnp.bfloat16), "rep", axis=1, tiled=True)
    served = select_rows(got_nbr.reshape(-1), updated).reshape(groups, nbr_cap, -1)
    returned = lax.all_to_all(served, "nodes", split_axis=0, concat_axis=0, tiled=True)
    fetched = returned.reshape(-1, updated.shape[1])[nbr_slot]
    gaps = ticks[:, None] - nbr_tick.astype(jnp.float32)
    time_enc = encode(gaps, freq, phase).reshape(-1, freq.shape[0]).astype(jnp.bfloat16)
    query = jnp.dot(updated[src_local], w_query, preferred_element_type=jnp.float32).astype(
        jnp.bfloat16
    )
    embed = attend(fetched, time_enc, query, w_keyval_mem, w_keyval_time)
    return (new_part, embed)


def solution(mesh):
    placed = (
        P("nodes", None),
        P("nodes"),
        P(("nodes", "rep")),
        P(("nodes", "rep"), None),
        P(("nodes", "rep")),
        P(("nodes", "rep")),
        P(("nodes", "rep"), None, None),
        P(("nodes", "rep"), None),
        P(("nodes", "rep"), None),
        P(),
        P(),
        P(),
        P(None, None, "rep"),
        P(None, None, "rep"),
        P(None, "rep"),
        P(),
        P(),
        P(),
    )
    return jax.shard_map(
        on_device,
        mesh=mesh,
        in_specs=placed,
        out_specs=(P("nodes", "rep"), P(("nodes", "rep"), None)),
        check_vma=False,
    )
```

```python
import math

import jax
import jax.numpy as jnp
from jax import lax
from jax.experimental import pallas as pl
from jax.experimental.pallas import tpu as pltpu
from jax.sharding import PartitionSpec as P

HEADS = 8
HEAD_DIM = 64


def encode(gaps, freq, phase):
    return jnp.cos(gaps[..., None] * freq + phase)


def place(owner, groups, capacity):
    onehot = (owner[:, None] == jnp.arange(groups, dtype=jnp.int32)[None, :]).astype(jnp.int32)
    before = jnp.cumsum(onehot, axis=0) - onehot
    rank = jnp.sum(before * onehot, axis=1)
    return owner * capacity + rank, onehot, rank


def split_pairs(v):
    return (v // 32).astype(jnp.bfloat16), (v % 32).astype(jnp.bfloat16)


def scatter_ids(onehot, rank, values, capacity):
    hi, lo = split_pairs(values + 1)
    at_rank = rank[:, None] == jnp.arange(capacity, dtype=jnp.int32)[None, :]
    cols = jnp.concatenate(
        [jnp.where(at_rank, hi[:, None], 0.0), jnp.where(at_rank, lo[:, None], 0.0)], axis=1
    ).astype(jnp.bfloat16)
    table = jnp.dot(onehot.T.astype(jnp.bfloat16), cols, preferred_element_type=jnp.float32)
    table = table.astype(jnp.int32)
    return table[:, :capacity] * 32 + table[:, capacity:] - 1


def select_rows(ids, table):
    hits = (ids[:, None] == jnp.arange(table.shape[0], dtype=jnp.int32)[None, :]).astype(table.dtype)
    return jnp.dot(hits, table, preferred_element_type=jnp.float32).astype(table.dtype)


def attend_kernel(fetched_ref, tenc_ref, q_ref, wm_ref, wt_ref, out_ref):
    f32, bf16 = jnp.float32, jnp.bfloat16
    block = q_ref.shape[0]
    rows = fetched_ref.shape[0]
    nbrs = rows // block
    width = q_ref.shape[1]
    kv_mem = jnp.dot(fetched_ref[...], wm_ref[...], preferred_element_type=f32).astype(bf16)
    kv_time = jnp.dot(tenc_ref[...], wt_ref[...], preferred_element_type=f32)
    keyval = kv_mem.astype(f32) + kv_time
    keys = keyval[:, :width]
    values = keyval[:, width:]
    query = q_ref[...].astype(f32)
    prod = (keys.reshape(block, nbrs, width) * query[:, None, :]).reshape(rows, width)
    lane = lax.broadcasted_iota(jnp.int32, (width, 128), 0)
    col = lax.broadcasted_iota(jnp.int32, (width, 128), 1)
    head_of = (lane // HEAD_DIM == col).astype(bf16)
    hi = prod.astype(bf16)
    lo = (prod - hi.astype(f32)).astype(bf16)
    scores = jnp.dot(hi, head_of, preferred_element_type=f32) + jnp.dot(
        lo, head_of, preferred_element_type=f32
    )
    scores = (scores / math.sqrt(HEAD_DIM)).reshape(block, nbrs, 128)
    top = jnp.max(scores, axis=1, keepdims=True)
    ex = jnp.exp(scores - top)
    weights = (ex / jnp.sum(ex, axis=1, keepdims=True)).reshape(rows, 128)
    row = lax.broadcasted_iota(jnp.int32, (128, width), 0)
    lane2 = lax.broadcasted_iota(jnp.int32, (128, width), 1)
    head_to = (lane2 // HEAD_DIM == row).astype(bf16)
    w_hi = weights.astype(bf16)
    w_lo = (weights - w_hi.astype(f32)).astype(bf16)
    spread = jnp.dot(w_hi, head_to, preferred_element_type=f32) + jnp.dot(
        w_lo, head_to, preferred_element_type=f32
    )
    mixed = jnp.sum((spread * values).reshape(block, nbrs, width), axis=1)
    out_ref[...] = mixed.astype(out_ref.dtype)


def attend(fetched, time_enc, query, w_keyval_mem, w_keyval_time, block=32):
    events, width = query.shape
    nbrs = fetched.shape[0] // events
    rows = block * nbrs
    return pl.pallas_call(
        attend_kernel,
        grid=(events // block,),
        in_specs=[
            pl.BlockSpec((rows, fetched.shape[1]), lambda i: (i, 0)),
            pl.BlockSpec((rows, time_enc.shape[1]), lambda i: (i, 0)),
            pl.BlockSpec((block, width), lambda i: (i, 0)),
            pl.BlockSpec(w_keyval_mem.shape, lambda i: (0, 0)),
            pl.BlockSpec(w_keyval_time.shape, lambda i: (0, 0)),
        ],
        out_specs=pl.BlockSpec((block, width), lambda i: (i, 0)),
        out_shape=jax.ShapeDtypeStruct((events, width), jnp.bfloat16),
    )(fetched, time_enc, query, w_keyval_mem, w_keyval_time)


def on_device(
    memory,
    last_tick,
    src_local,
    dst_owner,
    dst_local,
    event_tick,
    nbr_owner,
    nbr_local,
    nbr_tick,
    freq,
    phase,
    w_message,
    gru_input,
    gru_hidden,
    gru_bias,
    w_query,
    w_keyval_mem,
    w_keyval_time,
):
    groups = lax.axis_size("nodes")
    reps = lax.axis_size("rep")
    events = src_local.shape[0]
    rows_here = memory.shape[0]
    width_m = memory.shape[1]
    neighbours = nbr_local.shape[1]
    dst_cap = max(2, 2 * events // groups)
    nbr_cap = 2 * events * neighbours // groups
    dst_slot, _, _ = place(dst_owner[:, 0], groups, dst_cap)
    nbr_slot, nbr_hot, nbr_rank = place(nbr_owner.reshape(-1), groups, nbr_cap)
    mem_half = memory.astype(jnp.bfloat16)
    near_rows = mem_half[src_local]
    near_ticks = last_tick[src_local]
    ticks = event_tick.astype(jnp.float32)

    req = jnp.stack([dst_local, event_tick, near_ticks], axis=1)
    req_ints = (
        jnp.full((groups * dst_cap, 3), -1, jnp.int32)
        .at[dst_slot]
        .set(req)
        .reshape(groups, dst_cap * 3)
    )
    nbr_ids = scatter_ids(nbr_hot, nbr_rank, nbr_local.reshape(-1), nbr_cap)
    req_rows = (
        jnp.zeros((groups * dst_cap, width_m), jnp.bfloat16)
        .at[dst_slot]
        .set(near_rows)
        .reshape(groups, dst_cap, width_m)
    )
    ints_out = jnp.concatenate([req_ints, nbr_ids], axis=1)
    ints_in = lax.all_to_all(ints_out, "nodes", split_axis=0, concat_axis=0, tiled=True)
    rows_in = lax.all_to_all(req_rows, "nodes", split_axis=0, concat_axis=0, tiled=True)
    got = ints_in[:, : dst_cap * 3].reshape(groups * dst_cap, 3)
    got_nbr = ints_in[:, dst_cap * 3 :]
    got_dst = got[:, 0]
    got_tick = got[:, 1].astype(jnp.float32)
    got_src_tick = got[:, 2].astype(jnp.float32)
    safe_dst = jnp.maximum(got_dst, 0)
    far_src = rows_in.reshape(-1, width_m)
    own_dst = mem_half[safe_dst]
    own_dst_tick = last_tick[safe_dst].astype(jnp.float32)

    src_time = encode(got_tick - got_src_tick, freq, phase).astype(jnp.bfloat16)
    dst_time = encode(got_tick - own_dst_tick, freq, phase).astype(jnp.bfloat16)
    slots = far_src.shape[0]
    stacked = jnp.concatenate(
        [
            jnp.concatenate([far_src, own_dst, src_time], axis=1),
            jnp.concatenate([own_dst, far_src, dst_time], axis=1),
        ],
        axis=0,
    )
    messages = jax.nn.silu(jnp.dot(stacked, w_message, preferred_element_type=jnp.float32)).astype(
        jnp.bfloat16
    )
    msg_src_slots = messages[:slots]
    msg_dst = messages[slots:]
    back = lax.all_to_all(
        msg_src_slots.reshape(groups, dst_cap, -1), "nodes", split_axis=0, concat_axis=0, tiled=True
    )
    msg_src = back.reshape(-1, back.shape[2])[dst_slot]

    local_msgs = jnp.concatenate([msg_src, msg_dst], axis=0)
    local_ids = jnp.concatenate([src_local, got_dst], axis=0)
    id_hi, id_lo = split_pairs(local_ids + 1)
    id_rows = -(-2 * local_ids.shape[0] // width_m)
    id_rows = -(-id_rows // 16) * 16
    id_block = jnp.concatenate(
        [id_hi, id_lo, jnp.zeros((id_rows * width_m - 2 * local_ids.shape[0],), jnp.bfloat16)]
    ).reshape(id_rows, width_m)
    payload = jnp.concatenate([local_msgs, id_block], axis=0)
    parts = [payload]
    for shift in range(1, reps):
        pairs = [(i, (i + shift) % reps) for i in range(reps)]
        parts.append(lax.ppermute(payload, "rep", pairs))
    count = local_msgs.shape[0]
    all_msgs = jnp.concatenate([p[:count] for p in parts], axis=0)
    coded = jnp.stack([p[count:].reshape(-1)[: 2 * count] for p in parts]).astype(jnp.int32)
    all_ids = (coded[:, :count] * 32 + coded[:, count:] - 1).reshape(-1)
    row_ids = jnp.arange(rows_here, dtype=jnp.int32)[:, None]
    hits = row_ids == all_ids[None, :]
    sums = jnp.dot(hits.astype(jnp.bfloat16), all_msgs, preferred_element_type=jnp.float32)
    counts = jnp.sum(hits.astype(jnp.float32), axis=1)

    unit_width = gru_bias.shape[1]
    start = lax.axis_index("rep") * unit_width
    state_part = lax.dynamic_slice_in_dim(memory, start, unit_width, 1)
    mean = sums / jnp.maximum(counts, 1.0)[:, None]
    highest = lax.Precision.HIGHEST
    a_parts = jnp.einsum("rk,gku->gru", mean, gru_input, precision=highest)
    b_parts = jnp.einsum("rk,gku->gru", memory, gru_hidden, precision=highest)
    update = jax.nn.sigmoid(a_parts[0] + b_parts[0] + gru_bias[0])
    reset = jax.nn.sigmoid(a_parts[1] + b_parts[1] + gru_bias[1])
    cand = jnp.tanh(a_parts[2] + gru_bias[2] + reset * (b_parts[2] + gru_bias[3]))
    fresh = (1.0 - update) * cand + update * state_part
    new_part = jnp.where((counts > 0.0)[:, None], fresh, state_part)
    updated = lax.all_gather(new_part.astype(jnp.bfloat16), "rep", axis=1, tiled=True)
    served = select_rows(got_nbr.reshape(-1), updated).reshape(groups, nbr_cap, -1)
    returned = lax.all_to_all(served, "nodes", split_axis=0, concat_axis=0, tiled=True)
    fetched = select_rows(nbr_slot, returned.reshape(-1, updated.shape[1]))
    gaps = ticks[:, None] - nbr_tick.astype(jnp.float32)
    time_enc = encode(gaps, freq, phase).reshape(-1, freq.shape[0]).astype(jnp.bfloat16)
    query = jnp.dot(updated[src_local], w_query, preferred_element_type=jnp.float32).astype(
        jnp.bfloat16
    )
    embed = attend(fetched, time_enc, query, w_keyval_mem, w_keyval_time)
    return (new_part, embed)


def solution(mesh):
    placed = (
        P("nodes", None),
        P("nodes"),
        P(("nodes", "rep")),
        P(("nodes", "rep"), None),
        P(("nodes", "rep")),
        P(("nodes", "rep")),
        P(("nodes", "rep"), None, None),
        P(("nodes", "rep"), None),
        P(("nodes", "rep"), None),
        P(),
        P(),
        P(),
        P(None, None, "rep"),
        P(None, None, "rep"),
        P(None, "rep"),
        P(),
        P(),
        P(),
    )
    return jax.shard_map(
        on_device,
        mesh=mesh,
        in_specs=placed,
        out_specs=(P("nodes", "rep"), P(("nodes", "rep"), None)),
        check_vma=False,
    )
```

```python
import math

import jax
import jax.numpy as jnp
from jax import lax
from jax.experimental import pallas as pl
from jax.experimental.pallas import tpu as pltpu
from jax.sharding import PartitionSpec as P

HEADS = 8
HEAD_DIM = 64


def encode(gaps, freq, phase):
    return jnp.cos(gaps[..., None] * freq + phase)


def place(owner, groups, capacity):
    onehot = (owner[:, None] == jnp.arange(groups, dtype=jnp.int32)[None, :]).astype(jnp.int32)
    before = jnp.cumsum(onehot, axis=0) - onehot
    rank = jnp.sum(before * onehot, axis=1)
    return owner * capacity + rank, onehot, rank


def split_pairs(v):
    return (v // 32).astype(jnp.bfloat16), (v % 32).astype(jnp.bfloat16)


def scatter_ids(onehot, rank, values, capacity):
    hi, lo = split_pairs(values + 1)
    at_rank = rank[:, None] == jnp.arange(capacity, dtype=jnp.int32)[None, :]
    cols = jnp.concatenate(
        [jnp.where(at_rank, hi[:, None], 0.0), jnp.where(at_rank, lo[:, None], 0.0)], axis=1
    ).astype(jnp.bfloat16)
    table = jnp.dot(onehot.T.astype(jnp.bfloat16), cols, preferred_element_type=jnp.float32)
    table = table.astype(jnp.int32)
    return table[:, :capacity] * 32 + table[:, capacity:] - 1


def select_rows(ids, table):
    hits = (ids[:, None] == jnp.arange(table.shape[0], dtype=jnp.int32)[None, :]).astype(table.dtype)
    return jnp.dot(hits, table, preferred_element_type=jnp.float32).astype(table.dtype)


def attend_kernel(fetched_ref, tenc_ref, q_ref, wm_ref, wt_ref, out_ref):
    f32, bf16 = jnp.float32, jnp.bfloat16
    block = q_ref.shape[0]
    rows = fetched_ref.shape[0]
    nbrs = rows // block
    width = q_ref.shape[1]
    kv_mem = jnp.dot(fetched_ref[...], wm_ref[...], preferred_element_type=f32).astype(bf16)
    kv_time = jnp.dot(tenc_ref[...], wt_ref[...], preferred_element_type=f32)
    keyval = kv_mem.astype(f32) + kv_time
    keys = keyval[:, :width]
    values = keyval[:, width:]
    query = q_ref[...].astype(f32)
    prod = (keys.reshape(block, nbrs, width) * query[:, None, :]).reshape(rows, width)
    lane = lax.broadcasted_iota(jnp.int32, (width, 128), 0)
    col = lax.broadcasted_iota(jnp.int32, (width, 128), 1)
    head_of = (lane // HEAD_DIM == col).astype(bf16)
    hi = prod.astype(bf16)
    lo = (prod - hi.astype(f32)).astype(bf16)
    scores = jnp.dot(hi, head_of, preferred_element_type=f32) + jnp.dot(
        lo, head_of, preferred_element_type=f32
    )
    scores = (scores / math.sqrt(HEAD_DIM)).reshape(block, nbrs, 128)
    top = jnp.max(scores, axis=1, keepdims=True)
    ex = jnp.exp(scores - top)
    weights = (ex / jnp.sum(ex, axis=1, keepdims=True)).reshape(rows, 128)
    row = lax.broadcasted_iota(jnp.int32, (128, width), 0)
    lane2 = lax.broadcasted_iota(jnp.int32, (128, width), 1)
    head_to = (lane2 // HEAD_DIM == row).astype(bf16)
    w_hi = weights.astype(bf16)
    w_lo = (weights - w_hi.astype(f32)).astype(bf16)
    spread = jnp.dot(w_hi, head_to, preferred_element_type=f32) + jnp.dot(
        w_lo, head_to, preferred_element_type=f32
    )
    mixed = jnp.sum((spread * values).reshape(block, nbrs, width), axis=1)
    out_ref[...] = mixed.astype(out_ref.dtype)


def attend(fetched, time_enc, query, w_keyval_mem, w_keyval_time, block=64):
    events, width = query.shape
    nbrs = fetched.shape[0] // events
    rows = block * nbrs
    return pl.pallas_call(
        attend_kernel,
        grid=(events // block,),
        in_specs=[
            pl.BlockSpec((rows, fetched.shape[1]), lambda i: (i, 0)),
            pl.BlockSpec((rows, time_enc.shape[1]), lambda i: (i, 0)),
            pl.BlockSpec((block, width), lambda i: (i, 0)),
            pl.BlockSpec(w_keyval_mem.shape, lambda i: (0, 0)),
            pl.BlockSpec(w_keyval_time.shape, lambda i: (0, 0)),
        ],
        out_specs=pl.BlockSpec((block, width), lambda i: (i, 0)),
        out_shape=jax.ShapeDtypeStruct((events, width), jnp.bfloat16),
    )(fetched, time_enc, query, w_keyval_mem, w_keyval_time)


def on_device(
    memory,
    last_tick,
    src_local,
    dst_owner,
    dst_local,
    event_tick,
    nbr_owner,
    nbr_local,
    nbr_tick,
    freq,
    phase,
    w_message,
    gru_input,
    gru_hidden,
    gru_bias,
    w_query,
    w_keyval_mem,
    w_keyval_time,
):
    groups = lax.axis_size("nodes")
    reps = lax.axis_size("rep")
    events = src_local.shape[0]
    rows_here = memory.shape[0]
    width_m = memory.shape[1]
    neighbours = nbr_local.shape[1]
    dst_cap = max(2, 2 * events // groups)
    nbr_cap = 2 * events * neighbours // groups
    dst_slot, _, _ = place(dst_owner[:, 0], groups, dst_cap)
    nbr_slot, nbr_hot, nbr_rank = place(nbr_owner.reshape(-1), groups, nbr_cap)
    mem_half = memory.astype(jnp.bfloat16)
    near_rows = mem_half[src_local]
    near_ticks = last_tick[src_local]
    ticks = event_tick.astype(jnp.float32)

    req = jnp.stack([dst_local, event_tick, near_ticks], axis=1)
    req_ints = (
        jnp.full((groups * dst_cap, 3), -1, jnp.int32)
        .at[dst_slot]
        .set(req)
        .reshape(groups, dst_cap * 3)
    )
    nbr_ids = scatter_ids(nbr_hot, nbr_rank, nbr_local.reshape(-1), nbr_cap)
    req_rows = (
        jnp.zeros((groups * dst_cap, width_m), jnp.bfloat16)
        .at[dst_slot]
        .set(near_rows)
        .reshape(groups, dst_cap, width_m)
    )
    ints_out = jnp.concatenate([req_ints, nbr_ids], axis=1)
    ints_in = lax.all_to_all(ints_out, "nodes", split_axis=0, concat_axis=0, tiled=True)
    rows_in = lax.all_to_all(req_rows, "nodes", split_axis=0, concat_axis=0, tiled=True)
    got = ints_in[:, : dst_cap * 3].reshape(groups * dst_cap, 3)
    got_nbr = ints_in[:, dst_cap * 3 :]
    got_dst = got[:, 0]
    got_tick = got[:, 1].astype(jnp.float32)
    got_src_tick = got[:, 2].astype(jnp.float32)
    safe_dst = jnp.maximum(got_dst, 0)
    far_src = rows_in.reshape(-1, width_m)
    own_dst = mem_half[safe_dst]
    own_dst_tick = last_tick[safe_dst].astype(jnp.float32)

    src_time = encode(got_tick - got_src_tick, freq, phase).astype(jnp.bfloat16)
    dst_time = encode(got_tick - own_dst_tick, freq, phase).astype(jnp.bfloat16)
    slots = far_src.shape[0]
    stacked = jnp.concatenate(
        [
            jnp.concatenate([far_src, own_dst, src_time], axis=1),
            jnp.concatenate([own_dst, far_src, dst_time], axis=1),
        ],
        axis=0,
    )
    messages = jax.nn.silu(jnp.dot(stacked, w_message, preferred_element_type=jnp.float32)).astype(
        jnp.bfloat16
    )
    msg_src_slots = messages[:slots]
    msg_dst = messages[slots:]
    back = lax.all_to_all(
        msg_src_slots.reshape(groups, dst_cap, -1), "nodes", split_axis=0, concat_axis=0, tiled=True
    )
    msg_src = back.reshape(-1, back.shape[2])[dst_slot]

    local_msgs = jnp.concatenate([msg_src, msg_dst], axis=0)
    local_ids = jnp.concatenate([src_local, got_dst], axis=0)
    id_hi, id_lo = split_pairs(local_ids + 1)
    id_rows = -(-2 * local_ids.shape[0] // width_m)
    id_rows = -(-id_rows // 16) * 16
    id_block = jnp.concatenate(
        [id_hi, id_lo, jnp.zeros((id_rows * width_m - 2 * local_ids.shape[0],), jnp.bfloat16)]
    ).reshape(id_rows, width_m)
    payload = jnp.concatenate([local_msgs, id_block], axis=0)
    parts = [payload]
    for shift in range(1, reps):
        pairs = [(i, (i + shift) % reps) for i in range(reps)]
        parts.append(lax.ppermute(payload, "rep", pairs))
    count = local_msgs.shape[0]
    all_msgs = jnp.concatenate([p[:count] for p in parts], axis=0)
    coded = jnp.stack([p[count:].reshape(-1)[: 2 * count] for p in parts]).astype(jnp.int32)
    all_ids = (coded[:, :count] * 32 + coded[:, count:] - 1).reshape(-1)
    row_ids = jnp.arange(rows_here, dtype=jnp.int32)[:, None]
    hits = row_ids == all_ids[None, :]
    sums = jnp.dot(hits.astype(jnp.bfloat16), all_msgs, preferred_element_type=jnp.float32)
    counts = jnp.sum(hits.astype(jnp.float32), axis=1)

    unit_width = gru_bias.shape[1]
    start = lax.axis_index("rep") * unit_width
    state_part = lax.dynamic_slice_in_dim(memory, start, unit_width, 1)
    mean = sums / jnp.maximum(counts, 1.0)[:, None]
    highest = lax.Precision.HIGHEST
    a_parts = jnp.einsum("rk,gku->gru", mean, gru_input, precision=highest)
    b_parts = jnp.einsum("rk,gku->gru", memory, gru_hidden, precision=highest)
    update = jax.nn.sigmoid(a_parts[0] + b_parts[0] + gru_bias[0])
    reset = jax.nn.sigmoid(a_parts[1] + b_parts[1] + gru_bias[1])
    cand = jnp.tanh(a_parts[2] + gru_bias[2] + reset * (b_parts[2] + gru_bias[3]))
    fresh = (1.0 - update) * cand + update * state_part
    new_part = jnp.where((counts > 0.0)[:, None], fresh, state_part)
    updated = lax.all_gather(new_part.astype(jnp.bfloat16), "rep", axis=1, tiled=True)
    served = select_rows(got_nbr.reshape(-1), updated).reshape(groups, nbr_cap, -1)
    returned = lax.all_to_all(served, "nodes", split_axis=0, concat_axis=0, tiled=True)
    fetched = returned.reshape(-1, updated.shape[1])[nbr_slot]
    gaps = ticks[:, None] - nbr_tick.astype(jnp.float32)
    time_enc = encode(gaps, freq, phase).reshape(-1, freq.shape[0]).astype(jnp.bfloat16)
    query = jnp.dot(updated[src_local], w_query, preferred_element_type=jnp.float32).astype(
        jnp.bfloat16
    )
    embed = attend(fetched, time_enc, query, w_keyval_mem, w_keyval_time)
    return (new_part, embed)


def solution(mesh):
    placed = (
        P("nodes", None),
        P("nodes"),
        P(("nodes", "rep")),
        P(("nodes", "rep"), None),
        P(("nodes", "rep")),
        P(("nodes", "rep")),
        P(("nodes", "rep"), None, None),
        P(("nodes", "rep"), None),
        P(("nodes", "rep"), None),
        P(),
        P(),
        P(),
        P(None, None, "rep"),
        P(None, None, "rep"),
        P(None, "rep"),
        P(),
        P(),
        P(),
    )
    return jax.shard_map(
        on_device,
        mesh=mesh,
        in_specs=placed,
        out_specs=(P("nodes", "rep"), P(("nodes", "rep"), None)),
        check_vma=False,
    )
```

```python
import math

import jax
import jax.numpy as jnp
from jax import lax
from jax.experimental import pallas as pl
from jax.experimental.pallas import tpu as pltpu
from jax.sharding import PartitionSpec as P

HEADS = 8
HEAD_DIM = 64


def encode(gaps, freq, phase):
    return jnp.cos(gaps[..., None] * freq + phase)


def place(owner, groups, capacity):
    onehot = (owner[:, None] == jnp.arange(groups, dtype=jnp.int32)[None, :]).astype(jnp.int32)
    before = jnp.cumsum(onehot, axis=0) - onehot
    rank = jnp.sum(before * onehot, axis=1)
    return owner * capacity + rank, onehot, rank


def split_pairs(v):
    return (v // 32).astype(jnp.bfloat16), (v % 32).astype(jnp.bfloat16)


def scatter_ids(onehot, rank, values, capacity):
    hi, lo = split_pairs(values + 1)
    at_rank = rank[:, None] == jnp.arange(capacity, dtype=jnp.int32)[None, :]
    cols = jnp.concatenate(
        [jnp.where(at_rank, hi[:, None], 0.0), jnp.where(at_rank, lo[:, None], 0.0)], axis=1
    ).astype(jnp.bfloat16)
    table = jnp.dot(onehot.T.astype(jnp.bfloat16), cols, preferred_element_type=jnp.float32)
    table = table.astype(jnp.int32)
    return table[:, :capacity] * 32 + table[:, capacity:] - 1


def select_rows(ids, table):
    hits = (ids[:, None] == jnp.arange(table.shape[0], dtype=jnp.int32)[None, :]).astype(table.dtype)
    return jnp.dot(hits, table, preferred_element_type=jnp.float32).astype(table.dtype)


def attend_kernel(fetched_ref, tenc_ref, q_ref, wm_ref, wt_ref, out_ref):
    f32, bf16 = jnp.float32, jnp.bfloat16
    block = q_ref.shape[0]
    rows = fetched_ref.shape[0]
    nbrs = rows // block
    width = q_ref.shape[1]
    kv_mem = jnp.dot(fetched_ref[...], wm_ref[...], preferred_element_type=f32).astype(bf16)
    kv_time = jnp.dot(tenc_ref[...], wt_ref[...], preferred_element_type=f32)
    keyval = kv_mem.astype(f32) + kv_time
    keys = keyval[:, :width]
    values = keyval[:, width:]
    query = q_ref[...].astype(f32)
    prod = (keys.reshape(block, nbrs, width) * query[:, None, :]).reshape(rows, width)
    lane = lax.broadcasted_iota(jnp.int32, (width, 128), 0)
    col = lax.broadcasted_iota(jnp.int32, (width, 128), 1)
    head_of = (lane // HEAD_DIM == col).astype(bf16)
    hi = prod.astype(bf16)
    lo = (prod - hi.astype(f32)).astype(bf16)
    scores = jnp.dot(hi, head_of, preferred_element_type=f32) + jnp.dot(
        lo, head_of, preferred_element_type=f32
    )
    scores = (scores / math.sqrt(HEAD_DIM)).reshape(block, nbrs, 128)
    top = jnp.max(scores, axis=1, keepdims=True)
    ex = jnp.exp(scores - top)
    weights = (ex / jnp.sum(ex, axis=1, keepdims=True)).reshape(rows, 128)
    row = lax.broadcasted_iota(jnp.int32, (128, width), 0)
    lane2 = lax.broadcasted_iota(jnp.int32, (128, width), 1)
    head_to = (lane2 // HEAD_DIM == row).astype(bf16)
    w_hi = weights.astype(bf16)
    w_lo = (weights - w_hi.astype(f32)).astype(bf16)
    spread = jnp.dot(w_hi, head_to, preferred_element_type=f32) + jnp.dot(
        w_lo, head_to, preferred_element_type=f32
    )
    mixed = jnp.sum((spread * values).reshape(block, nbrs, width), axis=1)
    out_ref[...] = mixed.astype(out_ref.dtype)


def attend(fetched, time_enc, query, w_keyval_mem, w_keyval_time, block=64):
    events, width = query.shape
    nbrs = fetched.shape[0] // events
    rows = block * nbrs
    return pl.pallas_call(
        attend_kernel,
        grid=(events // block,),
        in_specs=[
            pl.BlockSpec((rows, fetched.shape[1]), lambda i: (i, 0)),
            pl.BlockSpec((rows, time_enc.shape[1]), lambda i: (i, 0)),
            pl.BlockSpec((block, width), lambda i: (i, 0)),
            pl.BlockSpec(w_keyval_mem.shape, lambda i: (0, 0)),
            pl.BlockSpec(w_keyval_time.shape, lambda i: (0, 0)),
        ],
        out_specs=pl.BlockSpec((block, width), lambda i: (i, 0)),
        out_shape=jax.ShapeDtypeStruct((events, width), jnp.bfloat16),
    )(fetched, time_enc, query, w_keyval_mem, w_keyval_time)


def on_device(
    memory,
    last_tick,
    src_local,
    dst_owner,
    dst_local,
    event_tick,
    nbr_owner,
    nbr_local,
    nbr_tick,
    freq,
    phase,
    w_message,
    gru_input,
    gru_hidden,
    gru_bias,
    w_query,
    w_keyval_mem,
    w_keyval_time,
):
    groups = lax.axis_size("nodes")
    reps = lax.axis_size("rep")
    events = src_local.shape[0]
    rows_here = memory.shape[0]
    width_m = memory.shape[1]
    neighbours = nbr_local.shape[1]
    dst_cap = max(2, 2 * events // groups)
    nbr_cap = 2 * events * neighbours // groups
    dst_slot, _, _ = place(dst_owner[:, 0], groups, dst_cap)
    nbr_slot, nbr_hot, nbr_rank = place(nbr_owner.reshape(-1), groups, nbr_cap)
    mem_half = memory.astype(jnp.bfloat16)
    near_rows = mem_half[src_local]
    near_ticks = last_tick[src_local]
    ticks = event_tick.astype(jnp.float32)

    req = jnp.stack([dst_local, event_tick, near_ticks], axis=1)
    req_ints = (
        jnp.full((groups * dst_cap, 3), -1, jnp.int32)
        .at[dst_slot]
        .set(req)
        .reshape(groups, dst_cap * 3)
    )
    nbr_ids = scatter_ids(nbr_hot, nbr_rank, nbr_local.reshape(-1), nbr_cap)
    req_rows = select_rows(
        jnp.full((groups * dst_cap,), -1, jnp.int32).at[dst_slot].set(jnp.arange(events, dtype=jnp.int32)),
        near_rows,
    ).reshape(groups, dst_cap, width_m)
    ints_out = jnp.concatenate([req_ints, nbr_ids], axis=1)
    ints_in = lax.all_to_all(ints_out, "nodes", split_axis=0, concat_axis=0, tiled=True)
    rows_in = lax.all_to_all(req_rows, "nodes", split_axis=0, concat_axis=0, tiled=True)
    got = ints_in[:, : dst_cap * 3].reshape(groups * dst_cap, 3)
    got_nbr = ints_in[:, dst_cap * 3 :]
    got_dst = got[:, 0]
    got_tick = got[:, 1].astype(jnp.float32)
    got_src_tick = got[:, 2].astype(jnp.float32)
    safe_dst = jnp.maximum(got_dst, 0)
    far_src = rows_in.reshape(-1, width_m)
    own_dst = mem_half[safe_dst]
    own_dst_tick = last_tick[safe_dst].astype(jnp.float32)

    src_time = encode(got_tick - got_src_tick, freq, phase).astype(jnp.bfloat16)
    dst_time = encode(got_tick - own_dst_tick, freq, phase).astype(jnp.bfloat16)
    slots = far_src.shape[0]
    stacked = jnp.concatenate(
        [
            jnp.concatenate([far_src, own_dst, src_time], axis=1),
            jnp.concatenate([own_dst, far_src, dst_time], axis=1),
        ],
        axis=0,
    )
    messages = jax.nn.silu(jnp.dot(stacked, w_message, preferred_element_type=jnp.float32)).astype(
        jnp.bfloat16
    )
    msg_src_slots = messages[:slots]
    msg_dst = messages[slots:]
    back = lax.all_to_all(
        msg_src_slots.reshape(groups, dst_cap, -1), "nodes", split_axis=0, concat_axis=0, tiled=True
    )
    msg_src = back.reshape(-1, back.shape[2])[dst_slot]

    local_msgs = jnp.concatenate([msg_src, msg_dst], axis=0)
    local_ids = jnp.concatenate([src_local, got_dst], axis=0)
    id_hi, id_lo = split_pairs(local_ids + 1)
    id_rows = -(-2 * local_ids.shape[0] // width_m)
    id_rows = -(-id_rows // 16) * 16
    id_block = jnp.concatenate(
        [id_hi, id_lo, jnp.zeros((id_rows * width_m - 2 * local_ids.shape[0],), jnp.bfloat16)]
    ).reshape(id_rows, width_m)
    payload = jnp.concatenate([local_msgs, id_block], axis=0)
    parts = [payload]
    for shift in range(1, reps):
        pairs = [(i, (i + shift) % reps) for i in range(reps)]
        parts.append(lax.ppermute(payload, "rep", pairs))
    count = local_msgs.shape[0]
    all_msgs = jnp.concatenate([p[:count] for p in parts], axis=0)
    coded = jnp.stack([p[count:].reshape(-1)[: 2 * count] for p in parts]).astype(jnp.int32)
    all_ids = (coded[:, :count] * 32 + coded[:, count:] - 1).reshape(-1)
    row_ids = jnp.arange(rows_here, dtype=jnp.int32)[:, None]
    hits = row_ids == all_ids[None, :]
    sums = jnp.dot(hits.astype(jnp.bfloat16), all_msgs, preferred_element_type=jnp.float32)
    counts = jnp.sum(hits.astype(jnp.float32), axis=1)

    unit_width = gru_bias.shape[1]
    start = lax.axis_index("rep") * unit_width
    state_part = lax.dynamic_slice_in_dim(memory, start, unit_width, 1)
    mean = sums / jnp.maximum(counts, 1.0)[:, None]
    highest = lax.Precision.HIGHEST
    a_parts = jnp.einsum("rk,gku->gru", mean, gru_input, precision=highest)
    b_parts = jnp.einsum("rk,gku->gru", memory, gru_hidden, precision=highest)
    update = jax.nn.sigmoid(a_parts[0] + b_parts[0] + gru_bias[0])
    reset = jax.nn.sigmoid(a_parts[1] + b_parts[1] + gru_bias[1])
    cand = jnp.tanh(a_parts[2] + gru_bias[2] + reset * (b_parts[2] + gru_bias[3]))
    fresh = (1.0 - update) * cand + update * state_part
    new_part = jnp.where((counts > 0.0)[:, None], fresh, state_part)
    updated = lax.all_gather(new_part.astype(jnp.bfloat16), "rep", axis=1, tiled=True)
    served = select_rows(got_nbr.reshape(-1), updated).reshape(groups, nbr_cap, -1)
    returned = lax.all_to_all(served, "nodes", split_axis=0, concat_axis=0, tiled=True)
    fetched = returned.reshape(-1, updated.shape[1])[nbr_slot]
    gaps = ticks[:, None] - nbr_tick.astype(jnp.float32)
    time_enc = encode(gaps, freq, phase).reshape(-1, freq.shape[0]).astype(jnp.bfloat16)
    query = jnp.dot(updated[src_local], w_query, preferred_element_type=jnp.float32).astype(
        jnp.bfloat16
    )
    embed = attend(fetched, time_enc, query, w_keyval_mem, w_keyval_time)
    return (new_part, embed)


def solution(mesh):
    placed = (
        P("nodes", None),
        P("nodes"),
        P(("nodes", "rep")),
        P(("nodes", "rep"), None),
        P(("nodes", "rep")),
        P(("nodes", "rep")),
        P(("nodes", "rep"), None, None),
        P(("nodes", "rep"), None),
        P(("nodes", "rep"), None),
        P(),
        P(),
        P(),
        P(None, None, "rep"),
        P(None, None, "rep"),
        P(None, "rep"),
        P(),
        P(),
        P(),
    )
    return jax.shard_map(
        on_device,
        mesh=mesh,
        in_specs=placed,
        out_specs=(P("nodes", "rep"), P(("nodes", "rep"), None)),
        check_vma=False,
    )
```
